128 devices in a mesh: req: 64 (over z, y, x_hi, core), tp: 2 (over x_lo).
Axes of the slice: x: 4 (x_hi: 2, x_lo: 2; x = x_hi * 2 + x_lo), y: 4, z: 4, core: 2. Of those that a mesh axis runs over, the one named last changes fastest.
Arguments:
- hidden_in: bfloat16 [131072, 1536], P(('req', 'tp')), may hold values from -30 to 30
- segment_ids: int32 [131072], P('req'), may hold values from 0 to 9, as said below
- page_owner: int32 [2048], P('req'), may hold values from 0 to 63, as said below
- norm_gain: bfloat16 [1536], replicated, may hold values from 0.099609375 to 1.8984375
- w_qkv: bfloat16 [1536, 1536], P(None, 'tp'), may hold values from -16 to 16
- w_out: bfloat16 [768, 1536], P('tp'), may hold values from -0.625 to 0.625
Outputs:
- hidden_out: bfloat16 [131072, 1536], P(('req', 'tp'))
- kv_cache: bfloat16 [2048, 4, 2, 6144], P('req', 'tp')
The draws below stay inside these ranges and needn't reach their ends.
Inputs may be any that keep to these rules, and one draw needn't show every extreme that they name: `segment_ids`: within a group the numbers never fall. 0 marks the shared prefix, which comes first with 128 to 512 tokens; 1 to 8 mark the requests (a request may be empty); 9 marks padding at the end. At least three quarters of each group's tokens are not padding, and some group has none. `page_owner`: for each page number p, the 64 groups name 64 different owners for their page p. A group names one owner for at most 1 of its pages.
All inputs are finite; a program needn't handle non-finite values.
Results may differ from the reference program's by a relative error of at most 0.0095.
Values may be sent and summed in bfloat16 or wider, within the bound.
No kernel may reach another device: no remote copies, remote signals or barrier semaphores. Data moves between devices by JAX's collectives and lax.ppermute only.
A program may use at most 128 MiB of HBM per device.

```python
import math
import jax
import jax.numpy as jnp
from jax import lax

D = 1536
HEAD = 96
HEADS_Q = 8
HEADS_KV = 4
PAGE = 64
REQS = 8
TOK_DEV = 2048
TOKENS = 131072
PAGES_DEV = 32
QKV_COLS = 1536
CACHE_PAGES = 2048
N_REQ = 64
N_TP = 2


def draw_hidden_in(key, part):
    key_main, key_rows, key_cols = jax.random.split(key, 3)
    base_values = jnp.clip(jax.random.normal(key_main, (TOKENS, D), jnp.float32), -5.0, 5.0)
    row_scale = jnp.exp(jax.random.uniform(key_rows, (TOKENS, 1), jnp.float32, math.log(0.3), math.log(3.0)))
    col_scale = jnp.exp(jax.random.uniform(key_cols, (1, D), jnp.float32, math.log(0.5), math.log(2.0)))
    return (base_values * row_scale * col_scale).astype(jnp.bfloat16)


def draw_w_qkv(key, part):
    key_query, key_key, key_value = jax.random.split(key, 3)
    spread = D ** (-0.5)
    query_cols = jnp.clip(jax.random.normal(key_query, (D, HEADS_Q, HEAD), jnp.float32), -5.0, 5.0) * spread
    key_cols = jnp.clip(jax.random.normal(key_key, (D, HEADS_KV, HEAD), jnp.float32), -5.0, 5.0) * spread
    value_cols = jnp.clip(jax.random.normal(key_value, (D, HEADS_KV, HEAD), jnp.float32), -5.0, 5.0) * spread
    query_block = query_cols.reshape(D, N_TP, HEADS_Q // N_TP * HEAD)
    key_block = key_cols.reshape(D, N_TP, HEADS_KV // N_TP * HEAD)
    value_block = value_cols.reshape(D, N_TP, HEADS_KV // N_TP * HEAD)
    joined = jnp.concatenate([query_block, key_block, value_block], axis=2)
    return joined.reshape(D, QKV_COLS).astype(jnp.bfloat16)


def draw_segment_ids(key, part):
    key_full, key_live, key_prefix, key_cuts = jax.random.split(key, 4)
    full_group = jax.random.randint(key_full, (), 0, N_REQ)
    groups = jnp.arange(N_REQ, dtype=jnp.int32)
    live_len = jax.random.randint(key_live, (N_REQ,), 3 * TOK_DEV // 4, TOK_DEV + 1)
    live_len = jnp.where(groups == full_group, TOK_DEV, live_len)
    prefix_len = jax.random.randint(key_prefix, (N_REQ,), TOK_DEV // 16, TOK_DEV // 4 + 1)
    suffix_len = live_len - prefix_len
    cut_points = jax.random.randint(key_cuts, (N_REQ, REQS - 1), 0, 1 << 30)
    cut_points = prefix_len[:, None] + cut_points % suffix_len[:, None]
    token_index = jnp.arange(TOK_DEV, dtype=jnp.int32)
    counted = jnp.sum((cut_points[:, None, :] <= token_index[None, :, None]).astype(jnp.int32), axis=2)
    segments = 1 + counted
    segments = jnp.where(token_index[None, :] < prefix_len[:, None], 0, segments)
    segments = jnp.where(token_index[None, :] >= live_len[:, None], REQS + 1, segments)
    return segments.reshape(TOKENS).astype(jnp.int32)


def draw_page_owner(key, part):
    key_offset, key_owner = jax.random.split(key)
    offsets = jax.random.permutation(key_offset, N_REQ).astype(jnp.int32)
    relabel = jax.random.permutation(key_owner, N_REQ).astype(jnp.int32)
    group_index = jnp.arange(N_REQ, dtype=jnp.int32)[:, None]
    page_index = jnp.arange(PAGES_DEV, dtype=jnp.int32)[None, :]
    shifted = (group_index + offsets[page_index % N_REQ]) % N_REQ
    return relabel[shifted].reshape(CACHE_PAGES).astype(jnp.int32)


def level_of(rng, dims, pieces, least, largest):
    level, own = 1.0, jax.random.fold_in(rng, 6)
    for dim, parts in pieces:
        draws = jnp.exp(jax.random.uniform(jax.random.fold_in(own, dim), (parts,), jnp.float32, least / len(pieces), largest / len(pieces)))
        level = level * jnp.repeat(draws, dims[dim] // parts).reshape([-1 if axis == dim else 1 for axis in range(len(dims))])
    return level


def noise(rng, dims, scale, reach, shards=(), kind=jnp.bfloat16):
    factor_of = level_of(rng, dims, shards, -0.22, 0.18) if shards else 1.0
    values = jax.random.normal(rng, dims, jnp.float32) * scale * factor_of
    return jnp.minimum(jnp.maximum(values, -reach), reach).astype(kind)


def setup_inputs(seed: int = 0) -> dict:
    arg_keys = jax.random.split(jax.random.key(seed), 7)
    return {
        "hidden_in": draw_hidden_in(jax.random.fold_in(arg_keys[6], 71), 0),
        "segment_ids": draw_segment_ids(jax.random.fold_in(arg_keys[6], 71), 0),
        "page_owner": draw_page_owner(jax.random.fold_in(arg_keys[6], 71), 0),
        "norm_gain": jnp.clip(1.0 + 0.18 * jax.random.normal(arg_keys[3], (D,), jnp.float32), 0.099609375, 1.8984375).astype(jnp.bfloat16),
        "w_qkv": draw_w_qkv(jax.random.fold_in(arg_keys[6], 71), 0),
        "w_out": noise(arg_keys[5], (HEADS_Q * HEAD, D), HEAD ** -0.5, 0.625, ((0, 2),)),
    }


rotary_base = 100000.0
norm_eps = 1e-05
masked_score = -1e+30

def positions_of(segments):
    length = segments.shape[0]
    counter = jnp.arange(length, dtype=jnp.int32)
    previous = jnp.concatenate([segments[:1] - 1, segments[:-1]])
    starts = lax.cummax(jnp.where(segments != previous, counter, 0), axis=0)
    prefix_len = jnp.sum((segments == 0).astype(jnp.int32))
    return counter - starts + jnp.where(segments > 0, prefix_len, 0)

def rotary_tables(positions, width):
    half_width = width // 2
    exponent = jnp.arange(half_width, dtype=jnp.float32) * (2.0 / width)
    inverse = jnp.power(jnp.float32(rotary_base), -exponent)
    angles = positions.astype(jnp.float32)[:, None] * inverse[None, :]
    return (jnp.cos(angles), jnp.sin(angles))

def rotate(vectors, cosine, sine_table):
    half_width = vectors.shape[-1] // 2
    front_half = vectors[..., :half_width]
    second = vectors[..., half_width:]
    cosine = cosine[:, None, :]
    sine_table = sine_table[:, None, :]
    return jnp.concatenate([front_half * cosine - second * sine_table, second * cosine + front_half * sine_table], axis=-1)

def normalize(token_rows, gain_vector):
    values = token_rows.astype(jnp.float32)
    inverse_root = lax.rsqrt(lax.optimization_barrier(jnp.mean(values * values, axis=-1, keepdims=True)) + norm_eps)
    return (values * inverse_root * gain_vector.astype(jnp.float32)).astype(jnp.bfloat16)

def dense_attention(queries, key_vectors, value_vectors, segments):
    row_count = queries.shape[0]
    group_ratio = HEADS_Q // HEADS_KV
    places = jnp.arange(row_count, dtype=jnp.int32)
    allowed = (places[None, :] <= places[:, None]) & ((segments[None, :] == segments[:, None]) | (segments[None, :] == 0))
    wide_keys = jnp.repeat(key_vectors.astype(jnp.float32), group_ratio, axis=1)
    wide_values = jnp.repeat(value_vectors.astype(jnp.float32), group_ratio, axis=1)
    raw_scores = jnp.einsum('qhd,khd->hqk', queries.astype(jnp.float32), wide_keys) * HEAD ** (-0.5)
    row_max = lax.optimization_barrier(jnp.max(jnp.where(allowed, raw_scores, masked_score), axis=-1, keepdims=True))
    weights = jnp.where(allowed, jnp.exp(raw_scores - row_max), 0.0)
    totals = lax.optimization_barrier(jnp.sum(weights, axis=-1))
    rounded = weights.astype(jnp.bfloat16)
    rounded = lax.optimization_barrier(rounded)
    mixed_sum = jnp.einsum('hqk,khd->qhd', rounded.astype(jnp.float32), wide_values)
    result = mixed_sum / jnp.transpose(totals)[:, :, None]
    return result.astype(jnp.bfloat16).reshape(row_count, HEADS_Q * HEAD)

def reference(hidden_in, segment_ids, page_owner, norm_gain, w_qkv, w_out):
    query_width = HEADS_Q // N_TP * HEAD
    kv_width = HEADS_KV // N_TP * HEAD
    per_block = query_width + 2 * kv_width
    blocked = w_qkv.reshape(D, N_TP, per_block)
    w_query = blocked[:, :, :query_width].reshape(D, HEADS_Q * HEAD)
    w_key = blocked[:, :, query_width:query_width + kv_width].reshape(D, HEADS_KV * HEAD)
    w_value = blocked[:, :, query_width + kv_width:].reshape(D, HEADS_KV * HEAD)

    def group_layer(inputs):
        token_rows, segments = inputs
        normed = normalize(token_rows, norm_gain)
        positions = positions_of(segments)
        cosine, sine_table = rotary_tables(positions, HEAD)
        queries = jnp.dot(normed, w_query, preferred_element_type=jnp.float32).reshape(TOK_DEV, HEADS_Q, HEAD)
        queries = rotate(queries, cosine, sine_table).astype(jnp.bfloat16)
        key_vectors = jnp.dot(normed, w_key, preferred_element_type=jnp.float32).reshape(TOK_DEV, HEADS_KV, HEAD)
        key_vectors = rotate(key_vectors, cosine, sine_table).astype(jnp.bfloat16)
        value_vectors = jnp.dot(normed, w_value, preferred_element_type=jnp.float32).astype(jnp.bfloat16).reshape(TOK_DEV, HEADS_KV, HEAD)
        queries, key_vectors, value_vectors = lax.optimization_barrier((queries, key_vectors, value_vectors))
        attended = dense_attention(queries, key_vectors, value_vectors, segments)
        projected = jnp.dot(attended, w_out, preferred_element_type=jnp.float32)
        result = (token_rows.astype(jnp.float32) + projected).astype(jnp.bfloat16)
        key_pages = key_vectors.reshape(PAGES_DEV, PAGE, HEADS_KV, HEAD).transpose(0, 2, 1, 3).reshape(PAGES_DEV, HEADS_KV, PAGE * HEAD)
        value_pages = value_vectors.reshape(PAGES_DEV, PAGE, HEADS_KV, HEAD).transpose(0, 2, 1, 3).reshape(PAGES_DEV, HEADS_KV, PAGE * HEAD)
        return (result, jnp.stack([key_pages, value_pages], axis=2))
    rows_all = hidden_in.reshape(N_REQ, TOK_DEV, D)
    segments_all = segment_ids.reshape(N_REQ, TOK_DEV)
    results, page_blocks = lax.map(group_layer, (rows_all, segments_all))
    live_pages = segments_all[:, ::PAGE] != REQS + 1
    owners = page_owner.reshape(N_REQ, PAGES_DEV)
    page_numbers = jnp.arange(PAGES_DEV, dtype=jnp.int32)[None, :]
    targets = jnp.where(live_pages, owners * PAGES_DEV + page_numbers, CACHE_PAGES).astype(jnp.int32)
    cache_rows = jnp.zeros((CACHE_PAGES, HEADS_KV, 2, PAGE * HEAD), jnp.bfloat16)
    cache_rows = cache_rows.at[targets.reshape(CACHE_PAGES)].set(page_blocks.reshape(CACHE_PAGES, HEADS_KV, 2, PAGE * HEAD), mode='drop')
    return (results.reshape(TOKENS, D), cache_rows)
```

```python
import math

import jax
import jax.numpy as jnp
from jax import lax
from jax.sharding import PartitionSpec as P

HEAD = 96
HEADS_Q = 8
HEADS_KV = 4
PAGE = 64
REQS = 8


rotary_base = 100000.0
norm_eps = 1e-05
masked_score = -1e30


def positions_of(segments):
    length = segments.shape[0]
    counter = jnp.arange(length, dtype=jnp.int32)
    previous = jnp.concatenate([segments[:1] - 1, segments[:-1]])
    starts = lax.cummax(jnp.where(segments != previous, counter, 0), axis=0)
    prefix_len = jnp.sum((segments == 0).astype(jnp.int32))
    return counter - starts + jnp.where(segments > 0, prefix_len, 0)


def rotary_tables(positions, width):
    half_width = width // 2
    exponent = jnp.arange(half_width, dtype=jnp.float32) * (2.0 / width)
    inverse = jnp.power(jnp.float32(rotary_base), -exponent)
    angles = positions.astype(jnp.float32)[:, None] * inverse[None, :]
    return (jnp.cos(angles), jnp.sin(angles))


def rotate(vectors, cosine, sine_table):
    half_width = vectors.shape[-1] // 2
    front_half = vectors[..., :half_width]
    second = vectors[..., half_width:]
    cosine = cosine[:, None, :]
    sine_table = sine_table[:, None, :]
    return jnp.concatenate(
        [front_half * cosine - second * sine_table, second * cosine + front_half * sine_table],
        axis=-1,
    )


def normalize(token_rows, gain_vector):
    values = token_rows.astype(jnp.float32)
    inverse_root = lax.rsqrt(jnp.mean(values * values, axis=-1, keepdims=True) + norm_eps)
    return (values * inverse_root * gain_vector.astype(jnp.float32)).astype(jnp.bfloat16)


def attend(queries, key_vectors, value_vectors, query_segments, key_segments, query_offset):
    query_count = queries.shape[0]
    query_heads = queries.shape[1]
    head_width = queries.shape[2]
    key_count = key_vectors.shape[0]
    key_heads = key_vectors.shape[1]
    group_ratio = query_heads // key_heads
    query_block = math.gcd(query_count, max(8, 1024 // query_heads))
    factor = head_width ** (-0.5)
    grouped = queries.reshape(
        query_count // query_block, query_block, key_heads, group_ratio, head_width
    )
    segment_blocks = query_segments.reshape(query_count // query_block, query_block)
    key_places = jnp.arange(key_count, dtype=jnp.int32)

    def one_block(inputs):
        block_queries, block_segments, block_number = inputs
        query_start = query_offset + block_number * query_block
        query_places = query_start + jnp.arange(query_block, dtype=jnp.int32)
        allowed = (key_places[None, :] <= query_places[:, None]) & (
            (key_segments[None, :] == block_segments[:, None]) | (key_segments[None, :] == 0)
        )
        raw_scores = (
            jnp.einsum(
                "qhgd,khd->hgqk", block_queries, key_vectors, preferred_element_type=jnp.float32
            )
            * factor
        )
        masked = jnp.where(allowed, raw_scores, masked_score)
        row_max = jnp.max(masked, axis=-1, keepdims=True)
        weights = jnp.where(allowed, jnp.exp(masked - row_max), 0.0)
        totals = jnp.sum(weights, axis=-1)
        mixed_sum = jnp.einsum(
            "hgqk,khd->qhgd",
            weights.astype(jnp.bfloat16),
            value_vectors,
            preferred_element_type=jnp.float32,
        )
        result = mixed_sum / jnp.transpose(totals, (2, 0, 1))[..., None]
        return result.astype(jnp.bfloat16).reshape(query_block, query_heads * head_width)

    numbers = jnp.arange(query_count // query_block, dtype=jnp.int32)
    outputs = lax.map(one_block, (grouped, segment_blocks, numbers))
    return outputs.reshape(query_count, query_heads * head_width)


def shards(hidden_in, segment_ids, page_owner, norm_gain, w_qkv, w_out):
    tp_count = lax.axis_size("tp")
    req_count = lax.axis_size("req")
    tp_index = lax.axis_index("tp")
    req_index = lax.axis_index("req")
    group_len = segment_ids.shape[0]
    half_len = hidden_in.shape[0]
    local_query = HEADS_Q // tp_count
    local_kv = HEADS_KV // tp_count
    query_width = local_query * HEAD
    kv_width = local_kv * HEAD
    swap = [(0, 1), (1, 0)]
    page_count = group_len // PAGE
    live_pages = segment_ids[::PAGE] != REQS + 1
    owner_code = jnp.where(live_pages, page_owner, -1)
    owner_all = lax.all_gather(owner_code, "req", axis=0, tiled=False)
    positions = positions_of(segment_ids)
    cosine, sine_table = rotary_tables(positions, HEAD)
    normed_own = normalize(hidden_in, norm_gain)
    normed_other = lax.ppermute(normed_own, "tp", swap)
    proj_own = jnp.dot(normed_own, w_qkv, preferred_element_type=jnp.float32)
    proj_other = jnp.dot(normed_other, w_qkv, preferred_element_type=jnp.float32)
    first = tp_index == 0
    projected = jnp.concatenate(
        [jnp.where(first, proj_own, proj_other), jnp.where(first, proj_other, proj_own)], axis=0
    )
    queries = rotate(
        projected[:, :query_width].reshape(group_len, local_query, HEAD), cosine, sine_table
    ).astype(jnp.bfloat16)
    keys_local = rotate(
        projected[:, query_width : query_width + kv_width].reshape(group_len, local_kv, HEAD),
        cosine,
        sine_table,
    ).astype(jnp.bfloat16)
    values_local = (
        projected[:, query_width + kv_width :]
        .reshape(group_len, local_kv, HEAD)
        .astype(jnp.bfloat16)
    )
    key_pages = keys_local.reshape(page_count, PAGE, local_kv, HEAD).transpose(0, 2, 1, 3)
    value_pages = values_local.reshape(page_count, PAGE, local_kv, HEAD).transpose(0, 2, 1, 3)
    page_data = jnp.stack([key_pages, value_pages], axis=2).reshape(
        page_count, local_kv * 2 * PAGE * HEAD
    )
    owner_ids = jnp.arange(req_count, dtype=jnp.int32)
    to_owner = owner_code[None, :] == owner_ids[:, None]
    send_index = jnp.argmax(to_owner, axis=1)
    send_pages = jnp.where(
        jnp.any(to_owner, axis=1)[:, None], jnp.take(page_data, send_index, axis=0), 0
    ).astype(jnp.bfloat16)
    received = lax.all_to_all(send_pages, "req", split_axis=0, concat_axis=0, tiled=True)
    page_numbers = jnp.arange(page_count, dtype=jnp.int32)
    from_group = owner_all == req_index
    from_group = from_group.T
    source_group = jnp.argmax(from_group, axis=1)
    cache_rows = jnp.where(
        jnp.any(from_group, axis=1)[:, None], jnp.take(received, source_group, axis=0), 0
    ).astype(jnp.bfloat16)
    attended = attend(queries, keys_local, values_local, segment_ids, segment_ids, 0)
    other_start = (1 - tp_index) * half_len
    own_start = tp_index * half_len
    attended_other = lax.dynamic_slice_in_dim(attended, other_start, half_len, axis=0)
    attended_own = lax.dynamic_slice_in_dim(attended, own_start, half_len, axis=0)
    partial_other = jnp.dot(attended_other, w_out, preferred_element_type=jnp.float32).astype(
        jnp.bfloat16
    )
    partial_in = lax.ppermute(partial_other, "tp", swap)
    partial_own = jnp.dot(attended_own, w_out, preferred_element_type=jnp.float32)
    hidden_out = (
        hidden_in.astype(jnp.float32) + partial_own + partial_in.astype(jnp.float32)
    ).astype(jnp.bfloat16)
    return (hidden_out, cache_rows.reshape(page_count, local_kv, 2, PAGE * HEAD))


def solution(mesh):
    placed = (P(("req", "tp"), None), P("req"), P("req"), P(), P(None, "tp"), P("tp", None))
    return jax.shard_map(
        shards,
        mesh=mesh,
        in_specs=placed,
        out_specs=(P(("req", "tp"), None), P("req", "tp", None, None)),
        check_vma=False,
    )
```

```python
import math

import jax
import jax.numpy as jnp
from jax import lax
from jax.sharding import PartitionSpec as P

HEAD = 96
HEADS_Q = 8
HEADS_KV = 4
PAGE = 64
REQS = 8


rotary_base = 100000.0
norm_eps = 1e-05
masked_score = -1e30


def positions_of(segments):
    length = segments.shape[0]
    counter = jnp.arange(length, dtype=jnp.int32)
    previous = jnp.concatenate([segments[:1] - 1, segments[:-1]])
    starts = lax.cummax(jnp.where(segments != previous, counter, 0), axis=0)
    prefix_len = jnp.sum((segments == 0).astype(jnp.int32))
    return counter - starts + jnp.where(segments > 0, prefix_len, 0)


def rotary_tables(positions, width):
    half_width = width // 2
    exponent = jnp.arange(half_width, dtype=jnp.float32) * (2.0 / width)
    inverse = jnp.power(jnp.float32(rotary_base), -exponent)
    angles = positions.astype(jnp.float32)[:, None] * inverse[None, :]
    return (jnp.cos(angles), jnp.sin(angles))


def rotate(vectors, cosine, sine_table):
    half_width = vectors.shape[-1] // 2
    front_half = vectors[..., :half_width]
    second = vectors[..., half_width:]
    cosine = cosine[:, None, :]
    sine_table = sine_table[:, None, :]
    return jnp.concatenate(
        [front_half * cosine - second * sine_table, second * cosine + front_half * sine_table],
        axis=-1,
    )


def normalize(token_rows, gain_vector):
    values = token_rows.astype(jnp.float32)
    inverse_root = lax.rsqrt(jnp.mean(values * values, axis=-1, keepdims=True) + norm_eps)
    return (values * inverse_root * gain_vector.astype(jnp.float32)).astype(jnp.bfloat16)


def attend(queries, key_vectors, value_vectors, query_segments, key_segments, query_offset):
    query_count = queries.shape[0]
    query_heads = queries.shape[1]
    head_width = queries.shape[2]
    key_count = key_vectors.shape[0]
    key_heads = key_vectors.shape[1]
    group_ratio = query_heads // key_heads
    query_block = math.gcd(query_count, max(8, 1024 // query_heads))
    factor = head_width ** (-0.5)
    grouped = queries.reshape(
        query_count // query_block, query_block, key_heads, group_ratio, head_width
    )
    segment_blocks = query_segments.reshape(query_count // query_block, query_block)
    key_places = jnp.arange(key_count, dtype=jnp.int32)

    def one_block(inputs):
        block_queries, block_segments, block_number = inputs
        query_start = query_offset + block_number * query_block
        query_places = query_start + jnp.arange(query_block, dtype=jnp.int32)
        allowed = (key_places[None, :] <= query_places[:, None]) & (
            (key_segments[None, :] == block_segments[:, None]) | (key_segments[None, :] == 0)
        )
        raw_scores = (
            jnp.einsum(
                "qhgd,khd->hgqk", block_queries, key_vectors, preferred_element_type=jnp.float32
            )
            * factor
        )
        masked = jnp.where(allowed, raw_scores, masked_score)
        row_max = jnp.max(masked, axis=-1, keepdims=True)
        weights = jnp.where(allowed, jnp.exp(masked - row_max), 0.0)
        totals = jnp.sum(weights, axis=-1)
        mixed_sum = jnp.einsum(
            "hgqk,khd->qhgd",
            weights.astype(jnp.bfloat16),
            value_vectors,
            preferred_element_type=jnp.float32,
        )
        result = mixed_sum / jnp.transpose(totals, (2, 0, 1))[..., None]
        return result.astype(jnp.bfloat16).reshape(query_block, query_heads * head_width)

    numbers = jnp.arange(query_count // query_block, dtype=jnp.int32)
    outputs = lax.map(one_block, (grouped, segment_blocks, numbers))
    return outputs.reshape(query_count, query_heads * head_width)


def piece(block_queries, key_vectors, value_vectors, allowed):
    raw_scores = (
        jnp.einsum(
            "qhgd,khd->hgqk", block_queries, key_vectors, preferred_element_type=jnp.float32
        )
        * HEAD ** (-0.5)
    )
    masked = jnp.where(allowed, raw_scores, masked_score)
    row_max = jnp.max(masked, axis=-1)
    weights = jnp.where(allowed, jnp.exp(masked - row_max[..., None]), 0.0)
    totals = jnp.sum(weights, axis=-1)
    mixed_sum = jnp.einsum(
        "hgqk,khd->qhgd", weights.astype(jnp.bfloat16), value_vectors, preferred_element_type=jnp.float32
    )
    return row_max, totals, mixed_sum


def merge(first, second):
    max_a, total_a, sum_a = first
    max_b, total_b, sum_b = second
    row_max = jnp.maximum(max_a, max_b)
    scale_a = jnp.exp(max_a - row_max)
    scale_b = jnp.exp(max_b - row_max)
    totals = total_a * scale_a + total_b * scale_b
    mixed = sum_a * jnp.transpose(scale_a, (2, 0, 1))[..., None] + sum_b * jnp.transpose(
        scale_b, (2, 0, 1)
    )[..., None]
    return row_max, totals, mixed


def finish(parts):
    _, totals, mixed = parts
    result = mixed / jnp.transpose(totals, (2, 0, 1))[..., None]
    return result.astype(jnp.bfloat16).reshape(result.shape[0], -1)


def allowed_of(query_segments, key_segments, query_places, key_places):
    return (key_places[None, :] <= query_places[:, None]) & (
        (key_segments[None, :] == query_segments[:, None]) | (key_segments[None, :] == 0)
    )


def project(normed, w_qkv, cosine, sine_table, local_query, local_kv):
    rows = normed.shape[0]
    query_width = local_query * HEAD
    kv_width = local_kv * HEAD
    projected = jnp.dot(normed, w_qkv, preferred_element_type=jnp.float32)
    queries = rotate(
        projected[:, :query_width].reshape(rows, local_query, HEAD), cosine, sine_table
    ).astype(jnp.bfloat16)
    keys = rotate(
        projected[:, query_width : query_width + kv_width].reshape(rows, local_kv, HEAD),
        cosine,
        sine_table,
    ).astype(jnp.bfloat16)
    values = projected[:, query_width + kv_width :].reshape(rows, local_kv, HEAD).astype(jnp.bfloat16)
    return queries.reshape(rows, local_kv, local_query // local_kv, HEAD), keys, values


def pages_of(keys, values):
    count = keys.shape[0] // PAGE
    local_kv = keys.shape[1]
    key_pages = keys.reshape(count, PAGE, local_kv, HEAD).transpose(0, 2, 1, 3)
    value_pages = values.reshape(count, PAGE, local_kv, HEAD).transpose(0, 2, 1, 3)
    return jnp.stack([key_pages, value_pages], axis=2).reshape(count, local_kv * 2 * PAGE * HEAD)


def shards(hidden_in, segment_ids, page_owner, norm_gain, w_qkv, w_out):
    tp_count = lax.axis_size("tp")
    req_count = lax.axis_size("req")
    tp_index = lax.axis_index("tp")
    group_len = segment_ids.shape[0]
    half_len = hidden_in.shape[0]
    local_query = HEADS_Q // tp_count
    local_kv = HEADS_KV // tp_count
    swap = [(0, 1), (1, 0)]
    block = 256
    blocks = half_len // block
    first = tp_index == 0
    own_start = tp_index * half_len
    other_start = (1 - tp_index) * half_len
    page_count = group_len // PAGE
    positions = positions_of(segment_ids)
    cosine, sine_table = rotary_tables(positions, HEAD)
    places = jnp.arange(group_len, dtype=jnp.int32)

    def rows_of(array, begin):
        return lax.dynamic_slice_in_dim(array, begin, half_len, axis=0)

    normed_own = normalize(hidden_in, norm_gain)
    normed_other = jnp.concatenate(
        [
            lax.ppermute(normed_own[c * block : (c + 1) * block], "tp", swap)
            for c in range(blocks)
        ],
        axis=0,
    )
    seg_own, seg_other = rows_of(segment_ids, own_start), rows_of(segment_ids, other_start)
    place_own, place_other = rows_of(places, own_start), rows_of(places, other_start)
    q_own, k_own, v_own = project(
        normed_own, w_qkv, rows_of(cosine, own_start), rows_of(sine_table, own_start), local_query, local_kv
    )
    q_other, k_other, v_other = project(
        normed_other, w_qkv, rows_of(cosine, other_start), rows_of(sine_table, other_start), local_query, local_kv
    )

    pages_own = pages_of(k_own, v_own)
    pages_other = pages_of(k_other, v_other)
    page_data = jnp.where(
        first,
        jnp.concatenate([pages_own, pages_other], axis=0),
        jnp.concatenate([pages_other, pages_own], axis=0),
    )
    live_pages = segment_ids[::PAGE] != REQS + 1
    owner_ids = jnp.arange(req_count, dtype=jnp.int32)
    page_numbers = jnp.arange(page_count, dtype=jnp.int32)
    to_owner = (page_owner[None, :] == owner_ids[:, None]) & live_pages[None, :]
    send_index = jnp.argmax(to_owner, axis=1)
    has_page = jnp.any(to_owner, axis=1)
    tag = jnp.where(has_page, send_index + 1, 0).astype(jnp.bfloat16)
    send_pages = jnp.concatenate(
        [
            jnp.where(has_page[:, None], jnp.take(page_data, send_index, axis=0), 0).astype(jnp.bfloat16),
            jnp.broadcast_to(tag[:, None], (req_count, 128)),
        ],
        axis=1,
    )
    received = lax.all_to_all(send_pages, "req", split_axis=0, concat_axis=0, tiled=True)
    payload = page_data.shape[1]
    received_ids = received[:, payload].astype(jnp.int32) - 1
    from_group = received_ids[None, :] == page_numbers[:, None]
    source_group = jnp.argmax(from_group, axis=1)
    cache_rows = jnp.where(
        jnp.any(from_group, axis=1)[:, None], jnp.take(received[:, :payload], source_group, axis=0), 0
    ).astype(jnp.bfloat16)

    def diag(queries, keys, values, segs, place, b):
        rows = slice(b * block, (b + 1) * block)
        cols = slice(0, (b + 1) * block)
        allowed = allowed_of(segs[rows], segs[cols], place[rows], place[cols])
        return piece(queries[rows], keys[cols], values[cols], allowed)

    cross_q = jnp.where(first, q_other, q_own)
    cross_k = jnp.where(first, k_own, k_other)
    cross_v = jnp.where(first, v_own, v_other)
    seg_first = segment_ids[:half_len]
    seg_second = segment_ids[half_len:]
    other_partials = []
    own_rows = []
    for b in range(blocks):
        rows = slice(b * block, (b + 1) * block)
        cross = piece(
            cross_q[rows],
            cross_k,
            cross_v,
            allowed_of(seg_second[rows], seg_first, places[half_len:][rows], places[:half_len]),
        )
        unseen = (
            jnp.full_like(cross[0], masked_score),
            jnp.zeros_like(cross[1]),
            jnp.zeros_like(cross[2]),
        )
        cross_other = tuple(jnp.where(first, c, u) for c, u in zip(cross, unseen))
        cross_own = tuple(jnp.where(first, u, c) for c, u in zip(cross, unseen))
        other_parts = merge(diag(q_other, k_other, v_other, seg_other, place_other, b), cross_other)
        own_parts = merge(diag(q_own, k_own, v_own, seg_own, place_own, b), cross_own)
        other_partials.append(
            lax.ppermute(
                jnp.dot(finish(other_parts), w_out, preferred_element_type=jnp.float32).astype(
                    jnp.bfloat16
                ),
                "tp",
                swap,
            )
        )
        own_rows.append(finish(own_parts))
    partial_in = jnp.concatenate(other_partials, axis=0)
    partial_own = jnp.dot(jnp.concatenate(own_rows, axis=0), w_out, preferred_element_type=jnp.float32)
    hidden_out = (
        hidden_in.astype(jnp.float32) + partial_own + partial_in.astype(jnp.float32)
    ).astype(jnp.bfloat16)
    return (hidden_out, cache_rows.reshape(page_count, local_kv, 2, PAGE * HEAD))


def solution(mesh):
    placed = (P(("req", "tp"), None), P("req"), P("req"), P(), P(None, "tp"), P("tp", None))
    return jax.shard_map(
        shards,
        mesh=mesh,
        in_specs=placed,
        out_specs=(P(("req", "tp"), None), P("req", "tp", None, None)),
        check_vma=False,
    )
```

```python
import math

import jax
import jax.numpy as jnp
from jax import lax
from jax.experimental import pallas as pl
from jax.experimental.pallas import tpu as pltpu
from jax.sharding import PartitionSpec as P

HEAD = 96
HEADS_Q = 8
HEADS_KV = 4
PAGE = 64
REQS = 8
BLOCK = 256


rotary_base = 100000.0
norm_eps = 1e-05
masked_score = -1e30


def positions_of(segments):
    length = segments.shape[0]
    counter = jnp.arange(length, dtype=jnp.int32)
    previous = jnp.concatenate([segments[:1] - 1, segments[:-1]])
    starts = lax.cummax(jnp.where(segments != previous, counter, 0), axis=0)
    prefix_len = jnp.sum((segments == 0).astype(jnp.int32))
    return counter - starts + jnp.where(segments > 0, prefix_len, 0)


def rotary_tables(positions, width):
    half_width = width // 2
    exponent = jnp.arange(half_width, dtype=jnp.float32) * (2.0 / width)
    inverse = jnp.power(jnp.float32(rotary_base), -exponent)
    angles = positions.astype(jnp.float32)[:, None] * inverse[None, :]
    return (jnp.cos(angles), jnp.sin(angles))


def rotate(vectors, cosine, sine_table):
    half_width = vectors.shape[-1] // 2
    front_half = vectors[..., :half_width]
    second = vectors[..., half_width:]
    cosine = cosine[:, None, :]
    sine_table = sine_table[:, None, :]
    return jnp.concatenate(
        [front_half * cosine - second * sine_table, second * cosine + front_half * sine_table],
        axis=-1,
    )


def normalize(token_rows, gain_vector):
    values = token_rows.astype(jnp.float32)
    inverse_root = lax.rsqrt(jnp.mean(values * values, axis=-1, keepdims=True) + norm_eps)
    return (values * inverse_root * gain_vector.astype(jnp.float32)).astype(jnp.bfloat16)


def flash_kernel(meta_ref, q_ref, k_ref, v_ref, segq_ref, segk_ref, o_ref, m_sc, l_sc, acc_sc):
    step = pl.program_id(0)
    query_block = meta_ref[0] + step
    prefix_blocks = meta_ref[1]
    low_block = meta_ref[2 + query_block]
    query_heads = q_ref.shape[0]
    group = query_heads // k_ref.shape[0]
    m_sc[...] = jnp.full(m_sc.shape, masked_score, jnp.float32)
    l_sc[...] = jnp.zeros(l_sc.shape, jnp.float32)
    acc_sc[...] = jnp.zeros(acc_sc.shape, jnp.float32)
    query_segments = segq_ref[...]
    rows = query_block * BLOCK + lax.broadcasted_iota(jnp.int32, (BLOCK, 1), 0)

    def body(key_block, carry):
        @pl.when((key_block < prefix_blocks) | (key_block >= low_block))
        def _():
            start = pl.multiple_of(key_block * BLOCK, BLOCK)
            key_segments = segk_ref[:, pl.ds(start, BLOCK)]
            cols = start + lax.broadcasted_iota(jnp.int32, (1, BLOCK), 1)
            allowed = (cols <= rows) & (
                (key_segments == query_segments) | (key_segments == 0)
            )
            for head in range(query_heads):
                kv_head = head // group
                keys = k_ref[kv_head, pl.ds(start, BLOCK), :]
                values = v_ref[kv_head, pl.ds(start, BLOCK), :]
                scores = lax.dot_general(
                    q_ref[head], keys, (((1,), (1,)), ((), ())),
                    preferred_element_type=jnp.float32,
                ) * (HEAD ** (-0.5))
                scores = jnp.where(allowed, scores, masked_score)
                m_prev = m_sc[head]
                m_new = jnp.maximum(m_prev, jnp.max(scores, axis=-1, keepdims=True))
                alpha = jnp.exp(m_prev - m_new)
                weights = jnp.where(allowed, jnp.exp(scores - m_new), 0.0)
                l_sc[head] = alpha * l_sc[head] + jnp.sum(weights, axis=-1, keepdims=True)
                acc_sc[head] = alpha * acc_sc[head] + jnp.dot(
                    weights.astype(jnp.bfloat16), values, preferred_element_type=jnp.float32
                )
                m_sc[head] = m_new
        return carry

    lax.fori_loop(0, query_block + 1, body, 0)
    for head in range(query_heads):
        o_ref[head] = (acc_sc[head] / l_sc[head]).astype(o_ref.dtype)


def flash_attention(meta, queries, keys, values, segments, steps, interpret=False):
    query_heads, length, _ = queries.shape
    kv_heads = keys.shape[0]
    grid_spec = pltpu.PrefetchScalarGridSpec(
        num_scalar_prefetch=1,
        grid=(steps,),
        in_specs=[
            pl.BlockSpec((query_heads, BLOCK, HEAD), lambda i, m: (0, m[0] + i, 0)),
            pl.BlockSpec((kv_heads, length, HEAD), lambda i, m: (0, 0, 0)),
            pl.BlockSpec((kv_heads, length, HEAD), lambda i, m: (0, 0, 0)),
            pl.BlockSpec((BLOCK, 1), lambda i, m: (m[0] + i, 0)),
            pl.BlockSpec((1, length), lambda i, m: (0, 0)),
        ],
        out_specs=pl.BlockSpec((query_heads, BLOCK, HEAD), lambda i, m: (0, i, 0)),
        scratch_shapes=[
            pltpu.VMEM((query_heads, BLOCK, 1), jnp.float32),
            pltpu.VMEM((query_heads, BLOCK, 1), jnp.float32),
            pltpu.VMEM((query_heads, BLOCK, HEAD), jnp.float32),
        ],
    )
    return pl.pallas_call(
        flash_kernel,
        grid_spec=grid_spec,
        out_shape=jax.ShapeDtypeStruct((query_heads, steps * BLOCK, HEAD), jnp.bfloat16),
        compiler_params=pltpu.CompilerParams(dimension_semantics=("arbitrary",)),
        interpret=interpret,
    )(meta, queries, keys, values, segments.reshape(length, 1), segments.reshape(1, length))


def block_meta(segments, base):
    length = segments.shape[0]
    counter = jnp.arange(length, dtype=jnp.int32)
    previous = jnp.concatenate([segments[:1] - 1, segments[:-1]])
    starts = lax.cummax(jnp.where(segments != previous, counter, 0), axis=0)
    prefix_len = jnp.sum((segments == 0).astype(jnp.int32))
    prefix_blocks = (prefix_len + BLOCK - 1) // BLOCK
    low = starts[::BLOCK] // BLOCK
    return jnp.concatenate([jnp.stack([base, prefix_blocks]).astype(jnp.int32), low.astype(jnp.int32)])


def project(normed, w_qkv, cosine, sine_table, local_query, local_kv):
    rows = normed.shape[0]
    query_width = local_query * HEAD
    kv_width = local_kv * HEAD
    projected = jnp.dot(normed, w_qkv, preferred_element_type=jnp.float32)
    queries = rotate(
        projected[:, :query_width].reshape(rows, local_query, HEAD), cosine, sine_table
    ).astype(jnp.bfloat16)
    keys = rotate(
        projected[:, query_width : query_width + kv_width].reshape(rows, local_kv, HEAD),
        cosine,
        sine_table,
    ).astype(jnp.bfloat16)
    values = projected[:, query_width + kv_width :].reshape(rows, local_kv, HEAD).astype(jnp.bfloat16)
    return queries, keys, values


def pages_of(keys, values):
    count = keys.shape[0] // PAGE
    local_kv = keys.shape[1]
    key_pages = keys.reshape(count, PAGE, local_kv, HEAD).transpose(0, 2, 1, 3)
    value_pages = values.reshape(count, PAGE, local_kv, HEAD).transpose(0, 2, 1, 3)
    return jnp.stack([key_pages, value_pages], axis=2).reshape(count, local_kv, 2, PAGE * HEAD)


def shards(hidden_in, segment_ids, page_owner, norm_gain, w_qkv, w_out):
    tp_count = lax.axis_size("tp")
    req_count = lax.axis_size("req")
    tp_index = lax.axis_index("tp")
    group_len = segment_ids.shape[0]
    half_len = hidden_in.shape[0]
    local_query = HEADS_Q // tp_count
    local_kv = HEADS_KV // tp_count
    swap = [(0, 1), (1, 0)]
    blocks = half_len // BLOCK
    first = tp_index == 0
    own_start = tp_index * half_len
    other_start = (1 - tp_index) * half_len
    page_count = group_len // PAGE
    positions = positions_of(segment_ids)
    cosine, sine_table = rotary_tables(positions, HEAD)

    def rows_of(array, begin):
        return lax.dynamic_slice_in_dim(array, begin, half_len, axis=0)

    def in_order(own, other):
        return jnp.where(
            first, jnp.concatenate([own, other], axis=0), jnp.concatenate([other, own], axis=0)
        )

    normed_own = normalize(hidden_in, norm_gain)
    normed_other = jnp.concatenate(
        [
            lax.ppermute(normed_own[c * BLOCK : (c + 1) * BLOCK], "tp", swap)
            for c in range(blocks)
        ],
        axis=0,
    )
    q_own, k_own, v_own = project(
        normed_own, w_qkv, rows_of(cosine, own_start), rows_of(sine_table, own_start), local_query, local_kv
    )
    q_other, k_other, v_other = project(
        normed_other, w_qkv, rows_of(cosine, other_start), rows_of(sine_table, other_start), local_query, local_kv
    )
    keys = in_order(k_own, k_other)
    values = in_order(v_own, v_other)

    page_data = pages_of(keys, values)
    live_pages = segment_ids[::PAGE] != REQS + 1
    owner_ids = jnp.arange(req_count, dtype=jnp.int32)
    page_numbers = jnp.arange(page_count, dtype=jnp.int32)
    to_owner = (page_owner[None, :] == owner_ids[:, None]) & live_pages[None, :]
    send_index = jnp.argmax(to_owner, axis=1)
    has_page = jnp.any(to_owner, axis=1)
    tag = jnp.where(has_page, send_index + 1, 0).astype(jnp.bfloat16)
    payload = page_data.shape[-1]
    send_pages = jnp.concatenate(
        [
            jnp.where(
                has_page[:, None, None, None], jnp.take(page_data, send_index, axis=0), 0
            ).astype(jnp.bfloat16),
            jnp.broadcast_to(tag[:, None, None, None], (req_count, local_kv, 2, 128)),
        ],
        axis=3,
    )
    received = lax.all_to_all(send_pages, "req", split_axis=0, concat_axis=0, tiled=True)
    received_ids = received[:, 0, 0, payload].astype(jnp.int32) - 1
    from_group = received_ids[None, :] == page_numbers[:, None]
    source_group = jnp.argmax(from_group, axis=1)
    cache_rows = jnp.where(
        jnp.any(from_group, axis=1)[:, None, None, None],
        jnp.take(received, source_group, axis=0)[..., :payload],
        0,
    ).astype(jnp.bfloat16)

    query_heads = in_order(q_own, q_other).transpose(1, 0, 2)
    key_heads = keys.transpose(1, 0, 2)
    value_heads = values.transpose(1, 0, 2)
    w_out_heads = w_out.reshape(local_query, HEAD, w_out.shape[1])

    def attend_half(start):
        meta = block_meta(segment_ids, (start // BLOCK).astype(jnp.int32))
        return flash_attention(meta, query_heads, key_heads, value_heads, segment_ids, blocks)

    attended_other = attend_half(other_start)
    partial_in = jnp.concatenate(
        [
            lax.ppermute(
                jnp.einsum(
                    "hqd,hdc->qc",
                    attended_other[:, c * BLOCK : (c + 1) * BLOCK],
                    w_out_heads,
                    preferred_element_type=jnp.float32,
                ).astype(jnp.bfloat16),
                "tp",
                swap,
            )
            for c in range(blocks)
        ],
        axis=0,
    )
    attended_own = attend_half(own_start)
    partial_own = jnp.einsum(
        "hqd,hdc->qc", attended_own, w_out_heads, preferred_element_type=jnp.float32
    )
    hidden_out = (
        hidden_in.astype(jnp.float32) + partial_own + partial_in.astype(jnp.float32)
    ).astype(jnp.bfloat16)
    return (hidden_out, cache_rows)


def solution(mesh):
    placed = (P(("req", "tp"), None), P("req"), P("req"), P(), P(None, "tp"), P("tp", None))
    return jax.shard_map(
        shards,
        mesh=mesh,
        in_specs=placed,
        out_specs=(P(("req", "tp"), None), P("req", "tp", None, None)),
        check_vma=False,
    )
```

```python
import math

import jax
import jax.numpy as jnp
from jax import lax
from jax.experimental import pallas as pl
from jax.experimental.pallas import tpu as pltpu
from jax.sharding import PartitionSpec as P

HEAD = 96
HEADS_Q = 8
HEADS_KV = 4
PAGE = 64
REQS = 8
BLOCK = 256


rotary_base = 100000.0
norm_eps = 1e-05
masked_score = -1e30


def positions_of(segments):
    length = segments.shape[0]
    counter = jnp.arange(length, dtype=jnp.int32)
    previous = jnp.concatenate([segments[:1] - 1, segments[:-1]])
    starts = lax.cummax(jnp.where(segments != previous, counter, 0), axis=0)
    prefix_len = jnp.sum((segments == 0).astype(jnp.int32))
    return counter - starts + jnp.where(segments > 0, prefix_len, 0)


def rotary_tables(positions, width):
    half_width = width // 2
    exponent = jnp.arange(half_width, dtype=jnp.float32) * (2.0 / width)
    inverse = jnp.power(jnp.float32(rotary_base), -exponent)
    angles = positions.astype(jnp.float32)[:, None] * inverse[None, :]
    return (jnp.cos(angles), jnp.sin(angles))


def rotate(vectors, cosine, sine_table):
    half_width = vectors.shape[-1] // 2
    front_half = vectors[..., :half_width]
    second = vectors[..., half_width:]
    cosine = cosine[:, None, :]
    sine_table = sine_table[:, None, :]
    return jnp.concatenate(
        [front_half * cosine - second * sine_table, second * cosine + front_half * sine_table],
        axis=-1,
    )


def normalize(token_rows, gain_vector):
    values = token_rows.astype(jnp.float32)
    inverse_root = lax.rsqrt(jnp.mean(values * values, axis=-1, keepdims=True) + norm_eps)
    return (values * inverse_root * gain_vector.astype(jnp.float32)).astype(jnp.bfloat16)


def flash_kernel(meta_ref, q_ref, kt_ref, v_ref, segq_ref, segk_ref, o_ref, m_sc, l_sc, acc_sc):
    step = pl.program_id(1)
    query_block = meta_ref[0] + step
    prefix_blocks = meta_ref[1]
    low_block = meta_ref[2 + query_block]
    group = q_ref.shape[0]
    m_sc[...] = jnp.full(m_sc.shape, masked_score, jnp.float32)
    l_sc[...] = jnp.zeros(l_sc.shape, jnp.float32)
    acc_sc[...] = jnp.zeros(acc_sc.shape, jnp.float32)
    queries = q_ref[...].reshape(group * BLOCK, HEAD)
    rows = query_block * BLOCK + lax.broadcasted_iota(jnp.int32, (BLOCK, 1), 0)
    rows = jnp.concatenate([rows] * group, axis=0)
    query_segments = jnp.concatenate([segq_ref[...]] * group, axis=0)

    def body(key_block, carry):
        @pl.when((key_block < prefix_blocks) | (key_block >= low_block))
        def _():
            start = pl.multiple_of(key_block * BLOCK, BLOCK)
            key_segments = segk_ref[:, pl.ds(start, BLOCK)]
            cols = start + lax.broadcasted_iota(jnp.int32, (1, BLOCK), 1)
            allowed = (cols <= rows) & ((key_segments == query_segments) | (key_segments == 0))
            scores = jnp.dot(
                queries, kt_ref[0, :, pl.ds(start, BLOCK)], preferred_element_type=jnp.float32
            ) * (HEAD ** (-0.5))
            scores = jnp.where(allowed, scores, masked_score)
            m_prev = m_sc[...]
            m_new = jnp.maximum(m_prev, jnp.max(scores, axis=-1, keepdims=True))
            alpha = jnp.exp(m_prev - m_new)
            weights = jnp.where(allowed, jnp.exp(scores - m_new), 0.0)
            l_sc[...] = alpha * l_sc[...] + jnp.sum(weights, axis=-1, keepdims=True)
            acc_sc[...] = alpha * acc_sc[...] + jnp.dot(
                weights.astype(jnp.bfloat16),
                v_ref[0, pl.ds(start, BLOCK), :],
                preferred_element_type=jnp.float32,
            )
            m_sc[...] = m_new
        return carry

    lax.fori_loop(0, query_block + 1, body, 0)
    o_ref[...] = (acc_sc[...] / l_sc[...]).reshape(group, BLOCK, HEAD).astype(o_ref.dtype)


def flash_attention(meta, queries, keys, values, segments, steps, interpret=False):
    query_heads, length, _ = queries.shape
    kv_heads = keys.shape[0]
    group = query_heads // kv_heads
    grid_spec = pltpu.PrefetchScalarGridSpec(
        num_scalar_prefetch=1,
        grid=(kv_heads, steps),
        in_specs=[
            pl.BlockSpec((group, BLOCK, HEAD), lambda h, i, m: (h, m[0] + i, 0)),
            pl.BlockSpec((1, HEAD, length), lambda h, i, m: (h, 0, 0)),
            pl.BlockSpec((1, length, HEAD), lambda h, i, m: (h, 0, 0)),
            pl.BlockSpec((BLOCK, 1), lambda h, i, m: (m[0] + i, 0)),
            pl.BlockSpec((1, length), lambda h, i, m: (0, 0)),
        ],
        out_specs=pl.BlockSpec((group, BLOCK, HEAD), lambda h, i, m: (h, i, 0)),
        scratch_shapes=[
            pltpu.VMEM((group * BLOCK, 1), jnp.float32),
            pltpu.VMEM((group * BLOCK, 1), jnp.float32),
            pltpu.VMEM((group * BLOCK, HEAD), jnp.float32),
        ],
    )
    return pl.pallas_call(
        flash_kernel,
        grid_spec=grid_spec,
        out_shape=jax.ShapeDtypeStruct((query_heads, steps * BLOCK, HEAD), jnp.bfloat16),
        compiler_params=pltpu.CompilerParams(dimension_semantics=("arbitrary", "arbitrary")),
        interpret=interpret,
    )(meta, queries, keys.transpose(0, 2, 1), values, segments.reshape(length, 1), segments.reshape(1, length))


def block_meta(segments, base):
    length = segments.shape[0]
    counter = jnp.arange(length, dtype=jnp.int32)
    previous = jnp.concatenate([segments[:1] - 1, segments[:-1]])
    starts = lax.cummax(jnp.where(segments != previous, counter, 0), axis=0)
    prefix_len = jnp.sum((segments == 0).astype(jnp.int32))
    prefix_blocks = (prefix_len + BLOCK - 1) // BLOCK
    low = starts[::BLOCK] // BLOCK
    return jnp.concatenate([jnp.stack([base, prefix_blocks]).astype(jnp.int32), low.astype(jnp.int32)])


def project(normed, w_qkv, cosine, sine_table, local_query, local_kv):
    rows = normed.shape[0]
    query_width = local_query * HEAD
    kv_width = local_kv * HEAD
    projected = jnp.dot(normed, w_qkv, preferred_element_type=jnp.float32)
    queries = rotate(
        projected[:, :query_width].reshape(rows, local_query, HEAD), cosine, sine_table
    ).astype(jnp.bfloat16)
    keys = rotate(
        projected[:, query_width : query_width + kv_width].reshape(rows, local_kv, HEAD),
        cosine,
        sine_table,
    ).astype(jnp.bfloat16)
    values = projected[:, query_width + kv_width :].reshape(rows, local_kv, HEAD).astype(jnp.bfloat16)
    return queries, keys, values


def pages_of(keys, values):
    count = keys.shape[0] // PAGE
    local_kv = keys.shape[1]
    key_pages = keys.reshape(count, PAGE, local_kv, HEAD).transpose(0, 2, 1, 3)
    value_pages = values.reshape(count, PAGE, local_kv, HEAD).transpose(0, 2, 1, 3)
    return jnp.stack([key_pages, value_pages], axis=2).reshape(count, local_kv, 2, PAGE * HEAD)


def shards(hidden_in, segment_ids, page_owner, norm_gain, w_qkv, w_out):
    tp_count = lax.axis_size("tp")
    req_count = lax.axis_size("req")
    tp_index = lax.axis_index("tp")
    group_len = segment_ids.shape[0]
    half_len = hidden_in.shape[0]
    local_query = HEADS_Q // tp_count
    local_kv = HEADS_KV // tp_count
    swap = [(0, 1), (1, 0)]
    blocks = half_len // BLOCK
    first = tp_index == 0
    own_start = tp_index * half_len
    other_start = (1 - tp_index) * half_len
    page_count = group_len // PAGE
    positions = positions_of(segment_ids)
    cosine, sine_table = rotary_tables(positions, HEAD)

    def rows_of(array, begin):
        return lax.dynamic_slice_in_dim(array, begin, half_len, axis=0)

    def in_order(own, other):
        return jnp.where(
            first, jnp.concatenate([own, other], axis=0), jnp.concatenate([other, own], axis=0)
        )

    normed_own = normalize(hidden_in, norm_gain)
    normed_other = jnp.concatenate(
        [
            lax.ppermute(normed_own[c * BLOCK : (c + 1) * BLOCK], "tp", swap)
            for c in range(blocks)
        ],
        axis=0,
    )
    q_own, k_own, v_own = project(
        normed_own, w_qkv, rows_of(cosine, own_start), rows_of(sine_table, own_start), local_query, local_kv
    )
    q_other, k_other, v_other = project(
        normed_other, w_qkv, rows_of(cosine, other_start), rows_of(sine_table, other_start), local_query, local_kv
    )
    keys = in_order(k_own, k_other)
    values = in_order(v_own, v_other)

    page_data = pages_of(keys, values)
    live_pages = segment_ids[::PAGE] != REQS + 1
    owner_ids = jnp.arange(req_count, dtype=jnp.int32)
    page_numbers = jnp.arange(page_count, dtype=jnp.int32)
    to_owner = (page_owner[None, :] == owner_ids[:, None]) & live_pages[None, :]
    send_index = jnp.argmax(to_owner, axis=1)
    has_page = jnp.any(to_owner, axis=1)
    tag = jnp.where(has_page, send_index + 1, 0).astype(jnp.bfloat16)
    payload = page_data.shape[-1]
    send_pages = jnp.concatenate(
        [
            jnp.where(
                has_page[:, None, None, None], jnp.take(page_data, send_index, axis=0), 0
            ).astype(jnp.bfloat16),
            jnp.broadcast_to(tag[:, None, None, None], (req_count, local_kv, 2, 128)),
        ],
        axis=3,
    )
    received = lax.all_to_all(send_pages, "req", split_axis=0, concat_axis=0, tiled=True)
    received_ids = received[:, 0, 0, payload].astype(jnp.int32) - 1
    from_group = received_ids[None, :] == page_numbers[:, None]
    source_group = jnp.argmax(from_group, axis=1)
    cache_rows = jnp.where(
        jnp.any(from_group, axis=1)[:, None, None, None],
        jnp.take(received, source_group, axis=0)[..., :payload],
        0,
    ).astype(jnp.bfloat16)

    query_heads = in_order(q_own, q_other).transpose(1, 0, 2)
    key_heads = keys.transpose(1, 0, 2)
    value_heads = values.transpose(1, 0, 2)
    link_partner = [
        (r * tp_count + t, (r ^ 2) * tp_count + (tp_count - 1 - t))
        for r in range(req_count)
        for t in range(tp_count)
    ]
    w_out_other = lax.ppermute(w_out, ("req", "tp"), link_partner)

    def attend_half(start):
        meta = block_meta(segment_ids, (start // BLOCK).astype(jnp.int32))
        attended = flash_attention(meta, query_heads, key_heads, value_heads, segment_ids, blocks)
        return attended.transpose(1, 0, 2).reshape(half_len, local_query * HEAD)

    attended_in = lax.ppermute(attend_half(other_start), "tp", swap)
    attended_own = attend_half(own_start)
    projected_out = jnp.dot(attended_own, w_out, preferred_element_type=jnp.float32) + jnp.dot(
        attended_in, w_out_other, preferred_element_type=jnp.float32
    )
    hidden_out = (hidden_in.astype(jnp.float32) + projected_out).astype(jnp.bfloat16)
    return (hidden_out, cache_rows)


def solution(mesh):
    placed = (P(("req", "tp"), None), P("req"), P("req"), P(), P(None, "tp"), P("tp", None))
    return jax.shard_map(
        shards,
        mesh=mesh,
        in_specs=placed,
        out_specs=(P(("req", "tp"), None), P("req", "tp", None, None)),
        check_vma=False,
    )
```

```python
import functools
import math

import jax
import jax.numpy as jnp
from jax import lax
from jax.experimental import pallas as pl
from jax.experimental.pallas import tpu as pltpu
from jax.sharding import PartitionSpec as P

HEAD = 96
HEADS_Q = 8
HEADS_KV = 4
PAGE = 64
REQS = 8
BLOCK = 256
KEY_BLOCK = 512


rotary_base = 100000.0
norm_eps = 1e-05
masked_score = -1e30


def positions_of(segments):
    length = segments.shape[0]
    counter = jnp.arange(length, dtype=jnp.int32)
    previous = jnp.concatenate([segments[:1] - 1, segments[:-1]])
    starts = lax.cummax(jnp.where(segments != previous, counter, 0), axis=0)
    prefix_len = jnp.sum((segments == 0).astype(jnp.int32))
    return counter - starts + jnp.where(segments > 0, prefix_len, 0)


def rotary_tables(positions, width):
    half_width = width // 2
    exponent = jnp.arange(half_width, dtype=jnp.float32) * (2.0 / width)
    inverse = jnp.power(jnp.float32(rotary_base), -exponent)
    angles = positions.astype(jnp.float32)[:, None] * inverse[None, :]
    return (jnp.cos(angles), jnp.sin(angles))


def rotate(vectors, cosine, sine_table):
    half_width = vectors.shape[-1] // 2
    front_half = vectors[..., :half_width]
    second = vectors[..., half_width:]
    cosine = cosine[:, None, :]
    sine_table = sine_table[:, None, :]
    return jnp.concatenate(
        [front_half * cosine - second * sine_table, second * cosine + front_half * sine_table],
        axis=-1,
    )


def normalize(token_rows, gain_vector):
    values = token_rows.astype(jnp.float32)
    inverse_root = lax.rsqrt(jnp.mean(values * values, axis=-1, keepdims=True) + norm_eps)
    return (values * inverse_root * gain_vector.astype(jnp.float32)).astype(jnp.bfloat16)


def flash_kernel(key_width, meta_ref, q_ref, kt_ref, v_ref, segq_ref, segk_ref, o_ref, m_sc, l_sc, acc_sc):
    step = pl.program_id(0)
    query_block = meta_ref[0] + step
    prefix_blocks = meta_ref[1]
    low_block = meta_ref[2 + query_block]
    kv_heads = kt_ref.shape[0]
    group = q_ref.shape[0] // kv_heads
    m_sc[...] = jnp.full(m_sc.shape, masked_score, jnp.float32)
    l_sc[...] = jnp.zeros(l_sc.shape, jnp.float32)
    acc_sc[...] = jnp.zeros(acc_sc.shape, jnp.float32)
    rows = query_block * BLOCK + lax.broadcasted_iota(jnp.int32, (BLOCK, 1), 0)
    query_segments = segq_ref[...]

    def body(key_block, carry):
        @pl.when((key_block < prefix_blocks) | (key_block >= low_block))
        def _():
            start = pl.multiple_of(key_block * key_width, key_width)
            key_segments = segk_ref[:, pl.ds(start, key_width)]
            cols = start + lax.broadcasted_iota(jnp.int32, (1, key_width), 1)
            allowed = (cols <= rows) & ((key_segments == query_segments) | (key_segments == 0))
            bias = jnp.where(allowed, 0.0, masked_score)
            for kv_head in range(kv_heads):
                queries = q_ref[kv_head * group : (kv_head + 1) * group].reshape(group * BLOCK, HEAD)
                scores = jnp.dot(
                    queries, kt_ref[kv_head, :, pl.ds(start, key_width)], preferred_element_type=jnp.float32
                ) * (HEAD ** (-0.5))
                scores = (scores.reshape(group, BLOCK, key_width) + bias[None]).reshape(group * BLOCK, key_width)
                m_prev = m_sc[kv_head]
                m_new = jnp.maximum(m_prev, jnp.max(scores, axis=-1, keepdims=True))
                alpha = jnp.exp(m_prev - m_new)
                weights = jnp.exp(scores - m_new)
                l_sc[kv_head] = alpha * l_sc[kv_head] + jnp.sum(weights, axis=-1, keepdims=True)
                acc_sc[kv_head] = alpha * acc_sc[kv_head] + jnp.dot(
                    weights.astype(jnp.bfloat16),
                    v_ref[kv_head, pl.ds(start, key_width), :],
                    preferred_element_type=jnp.float32,
                )
                m_sc[kv_head] = m_new
        return carry

    lax.fori_loop(0, ((query_block + 1) * BLOCK + key_width - 1) // key_width, body, 0)
    for kv_head in range(kv_heads):
        o_ref[kv_head * group : (kv_head + 1) * group] = (
            (acc_sc[kv_head] / l_sc[kv_head]).reshape(group, BLOCK, HEAD).astype(o_ref.dtype)
        )


def flash_attention(meta, queries, keys, values, segments, steps, key_width=KEY_BLOCK, interpret=False):
    query_heads, length, _ = queries.shape
    kv_heads = keys.shape[0]
    group = query_heads // kv_heads
    grid_spec = pltpu.PrefetchScalarGridSpec(
        num_scalar_prefetch=1,
        grid=(steps,),
        in_specs=[
            pl.BlockSpec((query_heads, BLOCK, HEAD), lambda i, m: (0, m[0] + i, 0)),
            pl.BlockSpec((kv_heads, HEAD, length), lambda i, m: (0, 0, 0)),
            pl.BlockSpec((kv_heads, length, HEAD), lambda i, m: (0, 0, 0)),
            pl.BlockSpec((BLOCK, 1), lambda i, m: (m[0] + i, 0)),
            pl.BlockSpec((1, length), lambda i, m: (0, 0)),
        ],
        out_specs=pl.BlockSpec((query_heads, BLOCK, HEAD), lambda i, m: (0, i, 0)),
        scratch_shapes=[
            pltpu.VMEM((kv_heads, group * BLOCK, 1), jnp.float32),
            pltpu.VMEM((kv_heads, group * BLOCK, 1), jnp.float32),
            pltpu.VMEM((kv_heads, group * BLOCK, HEAD), jnp.float32),
        ],
    )
    return pl.pallas_call(
        functools.partial(flash_kernel, key_width),
        grid_spec=grid_spec,
        out_shape=jax.ShapeDtypeStruct((query_heads, steps * BLOCK, HEAD), jnp.bfloat16),
        compiler_params=pltpu.CompilerParams(dimension_semantics=("arbitrary",)),
        interpret=interpret,
    )(meta, queries, keys.transpose(0, 2, 1), values, segments.reshape(length, 1), segments.reshape(1, length))


def block_meta(segments, base, key_width=KEY_BLOCK):
    length = segments.shape[0]
    counter = jnp.arange(length, dtype=jnp.int32)
    previous = jnp.concatenate([segments[:1] - 1, segments[:-1]])
    starts = lax.cummax(jnp.where(segments != previous, counter, 0), axis=0)
    prefix_len = jnp.sum((segments == 0).astype(jnp.int32))
    prefix_blocks = (prefix_len + key_width - 1) // key_width
    low = starts[::BLOCK] // key_width
    return jnp.concatenate([jnp.stack([base, prefix_blocks]).astype(jnp.int32), low.astype(jnp.int32)])


def project(normed, w_qkv, cosine, sine_table, local_query, local_kv):
    rows = normed.shape[0]
    query_width = local_query * HEAD
    kv_width = local_kv * HEAD
    projected = jnp.dot(normed, w_qkv, preferred_element_type=jnp.float32)
    queries = rotate(
        projected[:, :query_width].reshape(rows, local_query, HEAD), cosine, sine_table
    ).astype(jnp.bfloat16)
    keys = rotate(
        projected[:, query_width : query_width + kv_width].reshape(rows, local_kv, HEAD),
        cosine,
        sine_table,
    ).astype(jnp.bfloat16)
    values = projected[:, query_width + kv_width :].reshape(rows, local_kv, HEAD).astype(jnp.bfloat16)
    return queries, keys, values


def pages_of(keys, values):
    count = keys.shape[0] // PAGE
    local_kv = keys.shape[1]
    key_pages = keys.reshape(count, PAGE, local_kv, HEAD).transpose(0, 2, 1, 3)
    value_pages = values.reshape(count, PAGE, local_kv, HEAD).transpose(0, 2, 1, 3)
    return jnp.stack([key_pages, value_pages], axis=2).reshape(count, local_kv, 2, PAGE * HEAD)


def shards(hidden_in, segment_ids, page_owner, norm_gain, w_qkv, w_out):
    tp_count = lax.axis_size("tp")
    req_count = lax.axis_size("req")
    tp_index = lax.axis_index("tp")
    group_len = segment_ids.shape[0]
    half_len = hidden_in.shape[0]
    local_query = HEADS_Q // tp_count
    local_kv = HEADS_KV // tp_count
    swap = [(0, 1), (1, 0)]
    blocks = half_len // BLOCK
    first = tp_index == 0
    own_start = tp_index * half_len
    other_start = (1 - tp_index) * half_len
    page_count = group_len // PAGE
    positions = positions_of(segment_ids)
    cosine, sine_table = rotary_tables(positions, HEAD)

    def rows_of(array, begin):
        return lax.dynamic_slice_in_dim(array, begin, half_len, axis=0)

    def in_order(own, other):
        return jnp.where(
            first, jnp.concatenate([own, other], axis=0), jnp.concatenate([other, own], axis=0)
        )

    normed_own = normalize(hidden_in, norm_gain)
    normed_other = jnp.concatenate(
        [
            lax.ppermute(normed_own[c * BLOCK : (c + 1) * BLOCK], "tp", swap)
            for c in range(blocks)
        ],
        axis=0,
    )
    q_own, k_own, v_own = project(
        normed_own, w_qkv, rows_of(cosine, own_start), rows_of(sine_table, own_start), local_query, local_kv
    )
    q_other, k_other, v_other = project(
        normed_other, w_qkv, rows_of(cosine, other_start), rows_of(sine_table, other_start), local_query, local_kv
    )
    keys = in_order(k_own, k_other)
    values = in_order(v_own, v_other)

    page_data = pages_of(keys, values)
    live_pages = segment_ids[::PAGE] != REQS + 1
    owner_ids = jnp.arange(req_count, dtype=jnp.int32)
    page_numbers = jnp.arange(page_count, dtype=jnp.int32)
    to_owner = (page_owner[None, :] == owner_ids[:, None]) & live_pages[None, :]
    send_index = jnp.argmax(to_owner, axis=1)
    has_page = jnp.any(to_owner, axis=1)
    tag = jnp.where(has_page, send_index + 1, 0).astype(jnp.bfloat16)
    payload = page_data.shape[-1]
    send_pages = jnp.concatenate(
        [
            jnp.where(
                has_page[:, None, None, None], jnp.take(page_data, send_index, axis=0), 0
            ).astype(jnp.bfloat16),
            jnp.broadcast_to(tag[:, None, None, None], (req_count, local_kv, 2, 128)),
        ],
        axis=3,
    )
    received = lax.all_to_all(send_pages, "req", split_axis=0, concat_axis=0, tiled=True)
    received_ids = received[:, 0, 0, payload].astype(jnp.int32) - 1
    from_group = received_ids[None, :] == page_numbers[:, None]
    source_group = jnp.argmax(from_group, axis=1)
    cache_rows = jnp.where(
        jnp.any(from_group, axis=1)[:, None, None, None],
        jnp.take(received, source_group, axis=0)[..., :payload],
        0,
    ).astype(jnp.bfloat16)

    query_heads = in_order(q_own, q_other).transpose(1, 0, 2)
    key_heads = keys.transpose(1, 0, 2)
    value_heads = values.transpose(1, 0, 2)
    link_partner = [
        (r * tp_count + t, (r ^ 2) * tp_count + (tp_count - 1 - t))
        for r in range(req_count)
        for t in range(tp_count)
    ]
    w_out_other = lax.ppermute(w_out, ("req", "tp"), link_partner)

    def attend_half(start):
        meta = block_meta(segment_ids, (start // BLOCK).astype(jnp.int32))
        attended = flash_attention(meta, query_heads, key_heads, value_heads, segment_ids, blocks)
        return attended.transpose(1, 0, 2).reshape(half_len, local_query * HEAD)

    attended_in = lax.ppermute(attend_half(other_start), "tp", swap)
    attended_own = attend_half(own_start)
    projected_out = jnp.dot(attended_own, w_out, preferred_element_type=jnp.float32) + jnp.dot(
        attended_in, w_out_other, preferred_element_type=jnp.float32
    )
    hidden_out = (hidden_in.astype(jnp.float32) + projected_out).astype(jnp.bfloat16)
    return (hidden_out, cache_rows)


def solution(mesh):
    placed = (P(("req", "tp"), None), P("req"), P("req"), P(), P(None, "tp"), P("tp", None))
    return jax.shard_map(
        shards,
        mesh=mesh,
        in_specs=placed,
        out_specs=(P(("req", "tp"), None), P("req", "tp", None, None)),
        check_vma=False,
    )
```

```python
import functools
import math

import jax
import jax.numpy as jnp
from jax import lax
from jax.experimental import pallas as pl
from jax.experimental.pallas import tpu as pltpu
from jax.sharding import PartitionSpec as P

HEAD = 96
HEADS_Q = 8
HEADS_KV = 4
PAGE = 64
REQS = 8
BLOCK = 256
KEY_BLOCK = 512


rotary_base = 100000.0
norm_eps = 1e-05
masked_score = -1e30


def positions_of(segments):
    length = segments.shape[0]
    counter = jnp.arange(length, dtype=jnp.int32)
    previous = jnp.concatenate([segments[:1] - 1, segments[:-1]])
    starts = lax.cummax(jnp.where(segments != previous, counter, 0), axis=0)
    prefix_len = jnp.sum((segments == 0).astype(jnp.int32))
    return counter - starts + jnp.where(segments > 0, prefix_len, 0)


def rotary_tables(positions, width):
    half_width = width // 2
    exponent = jnp.arange(half_width, dtype=jnp.float32) * (2.0 / width)
    inverse = jnp.power(jnp.float32(rotary_base), -exponent)
    angles = positions.astype(jnp.float32)[:, None] * inverse[None, :]
    return (jnp.cos(angles), jnp.sin(angles))


def rotate(vectors, cosine, sine_table):
    half_width = vectors.shape[-1] // 2
    front_half = vectors[..., :half_width]
    second = vectors[..., half_width:]
    cosine = cosine[:, None, :]
    sine_table = sine_table[:, None, :]
    return jnp.concatenate(
        [front_half * cosine - second * sine_table, second * cosine + front_half * sine_table],
        axis=-1,
    )


def normalize(token_rows, gain_vector):
    values = token_rows.astype(jnp.float32)
    inverse_root = lax.rsqrt(jnp.mean(values * values, axis=-1, keepdims=True) + norm_eps)
    return (values * inverse_root * gain_vector.astype(jnp.float32)).astype(jnp.bfloat16)


def flash_kernel(key_width, meta_ref, q_ref, kt_ref, v_ref, segq_ref, segk_ref, o_ref, m_sc, l_sc, acc_sc):
    step = pl.program_id(0)
    query_block = meta_ref[0] + step
    prefix_blocks = meta_ref[1]
    low_block = meta_ref[2 + query_block]
    kv_heads = kt_ref.shape[0]
    group = q_ref.shape[0] // kv_heads
    m_sc[...] = jnp.full(m_sc.shape, masked_score, jnp.float32)
    l_sc[...] = jnp.zeros(l_sc.shape, jnp.float32)
    acc_sc[...] = jnp.zeros(acc_sc.shape, jnp.float32)
    rows = query_block * BLOCK + lax.broadcasted_iota(jnp.int32, (BLOCK, 1), 0)
    query_segments = segq_ref[...]

    def body(key_block, carry):
        @pl.when((key_block < prefix_blocks) | (key_block >= low_block))
        def _():
            start = pl.multiple_of(key_block * key_width, key_width)
            key_segments = segk_ref[:, pl.ds(start, key_width)]
            cols = start + lax.broadcasted_iota(jnp.int32, (1, key_width), 1)
            allowed = (cols <= rows) & ((key_segments == query_segments) | (key_segments == 0))
            bias = jnp.where(allowed, 0.0, masked_score)
            for kv_head in range(kv_heads):
                queries = q_ref[kv_head * group : (kv_head + 1) * group].reshape(group * BLOCK, HEAD)
                scores = jnp.dot(
                    queries, kt_ref[kv_head, :, pl.ds(start, key_width)], preferred_element_type=jnp.float32
                ) * (HEAD ** (-0.5))
                scores = (scores.reshape(group, BLOCK, key_width) + bias[None]).reshape(group * BLOCK, key_width)
                m_prev = m_sc[kv_head]
                m_new = jnp.maximum(m_prev, jnp.max(scores, axis=-1, keepdims=True))
                alpha = jnp.exp(m_prev - m_new)
                weights = jnp.exp(scores - m_new)
                l_sc[kv_head] = alpha * l_sc[kv_head] + jnp.sum(weights, axis=-1, keepdims=True)
                acc_sc[kv_head] = alpha * acc_sc[kv_head] + jnp.dot(
                    weights.astype(jnp.bfloat16),
                    v_ref[kv_head, pl.ds(start, key_width), :],
                    preferred_element_type=jnp.float32,
                )
                m_sc[kv_head] = m_new
        return carry

    lax.fori_loop(0, ((query_block + 1) * BLOCK + key_width - 1) // key_width, body, 0)
    for kv_head in range(kv_heads):
        o_ref[kv_head * group : (kv_head + 1) * group] = (
            (acc_sc[kv_head] / l_sc[kv_head]).reshape(group, BLOCK, HEAD).astype(o_ref.dtype)
        )


def flash_attention(meta, queries, keys, values, segments, steps, key_width=KEY_BLOCK, interpret=False):
    query_heads, length, _ = queries.shape
    kv_heads = keys.shape[0]
    group = query_heads // kv_heads
    grid_spec = pltpu.PrefetchScalarGridSpec(
        num_scalar_prefetch=1,
        grid=(steps,),
        in_specs=[
            pl.BlockSpec((query_heads, BLOCK, HEAD), lambda i, m: (0, m[0] + i, 0)),
            pl.BlockSpec((kv_heads, HEAD, length), lambda i, m: (0, 0, 0)),
            pl.BlockSpec((kv_heads, length, HEAD), lambda i, m: (0, 0, 0)),
            pl.BlockSpec((BLOCK, 1), lambda i, m: (m[0] + i, 0)),
            pl.BlockSpec((1, length), lambda i, m: (0, 0)),
        ],
        out_specs=pl.BlockSpec((query_heads, BLOCK, HEAD), lambda i, m: (0, i, 0)),
        scratch_shapes=[
            pltpu.VMEM((kv_heads, group * BLOCK, 1), jnp.float32),
            pltpu.VMEM((kv_heads, group * BLOCK, 1), jnp.float32),
            pltpu.VMEM((kv_heads, group * BLOCK, HEAD), jnp.float32),
        ],
    )
    return pl.pallas_call(
        functools.partial(flash_kernel, key_width),
        grid_spec=grid_spec,
        out_shape=jax.ShapeDtypeStruct((query_heads, steps * BLOCK, HEAD), jnp.bfloat16),
        compiler_params=pltpu.CompilerParams(dimension_semantics=("arbitrary",)),
        interpret=interpret,
    )(meta, queries, keys.transpose(0, 2, 1), values, segments.reshape(length, 1), segments.reshape(1, length))


def block_meta(segments, base, key_width=KEY_BLOCK):
    length = segments.shape[0]
    counter = jnp.arange(length, dtype=jnp.int32)
    previous = jnp.concatenate([segments[:1] - 1, segments[:-1]])
    starts = lax.cummax(jnp.where(segments != previous, counter, 0), axis=0)
    prefix_len = jnp.sum((segments == 0).astype(jnp.int32))
    prefix_blocks = (prefix_len + key_width - 1) // key_width
    low = starts[::BLOCK] // key_width
    return jnp.concatenate([jnp.stack([base, prefix_blocks]).astype(jnp.int32), low.astype(jnp.int32)])


def project(normed, w_qkv, cosine, sine_table, local_query, local_kv):
    rows = normed.shape[0]
    query_width = local_query * HEAD
    kv_width = local_kv * HEAD
    projected = jnp.dot(normed, w_qkv, preferred_element_type=jnp.float32)
    queries = rotate(
        projected[:, :query_width].reshape(rows, local_query, HEAD), cosine, sine_table
    ).astype(jnp.bfloat16)
    keys = rotate(
        projected[:, query_width : query_width + kv_width].reshape(rows, local_kv, HEAD),
        cosine,
        sine_table,
    ).astype(jnp.bfloat16)
    values = projected[:, query_width + kv_width :].reshape(rows, local_kv, HEAD).astype(jnp.bfloat16)
    return queries, keys, values


def shards(hidden_in, segment_ids, page_owner, norm_gain, w_qkv, w_out):
    tp_count = lax.axis_size("tp")
    req_count = lax.axis_size("req")
    tp_index = lax.axis_index("tp")
    group_len = segment_ids.shape[0]
    half_len = hidden_in.shape[0]
    local_query = HEADS_Q // tp_count
    local_kv = HEADS_KV // tp_count
    swap = [(0, 1), (1, 0)]
    blocks = half_len // BLOCK
    first = tp_index == 0
    own_start = tp_index * half_len
    other_start = (1 - tp_index) * half_len
    page_count = group_len // PAGE
    positions = positions_of(segment_ids)
    cosine, sine_table = rotary_tables(positions, HEAD)

    def rows_of(array, begin):
        return lax.dynamic_slice_in_dim(array, begin, half_len, axis=0)

    def in_order(own, other):
        return jnp.where(
            first, jnp.concatenate([own, other], axis=0), jnp.concatenate([other, own], axis=0)
        )

    normed_own = normalize(hidden_in, norm_gain)
    normed_other = jnp.concatenate(
        [
            lax.ppermute(normed_own[c * BLOCK : (c + 1) * BLOCK], "tp", swap)
            for c in range(blocks)
        ],
        axis=0,
    )
    q_own, k_own, v_own = project(
        normed_own, w_qkv, rows_of(cosine, own_start), rows_of(sine_table, own_start), local_query, local_kv
    )
    q_other, k_other, v_other = project(
        normed_other, w_qkv, rows_of(cosine, other_start), rows_of(sine_table, other_start), local_query, local_kv
    )
    keys = in_order(k_own, k_other)
    values = in_order(v_own, v_other)

    token_pages = jnp.stack([keys, values], axis=2).reshape(page_count, PAGE, local_kv * 2 * HEAD)
    live_pages = segment_ids[::PAGE] != REQS + 1
    owner_ids = jnp.arange(req_count, dtype=jnp.int32)
    page_numbers = jnp.arange(page_count, dtype=jnp.int32)
    to_owner = (page_owner[None, :] == owner_ids[:, None]) & live_pages[None, :]
    send_index = jnp.argmax(to_owner, axis=1)
    has_page = jnp.any(to_owner, axis=1)
    tag = jnp.where(has_page, send_index + 1, 0).astype(jnp.bfloat16)
    tag_rows = 16
    send_pages = jnp.concatenate(
        [
            jnp.where(has_page[:, None, None], jnp.take(token_pages, send_index, axis=0), 0).astype(
                jnp.bfloat16
            ),
            jnp.broadcast_to(tag[:, None, None], (req_count, tag_rows, token_pages.shape[2])),
        ],
        axis=1,
    )
    received = lax.all_to_all(send_pages, "req", split_axis=0, concat_axis=0, tiled=True)
    received_ids = received[:, PAGE, 0].astype(jnp.int32) - 1
    from_group = received_ids[None, :] == page_numbers[:, None]
    source_group = jnp.argmax(from_group, axis=1)
    placed = jnp.where(
        jnp.any(from_group, axis=1)[:, None, None],
        jnp.take(received, source_group, axis=0)[:, :PAGE],
        0,
    ).astype(jnp.bfloat16)
    cache_rows = (
        placed.reshape(page_count, PAGE, local_kv, 2, HEAD)
        .transpose(0, 2, 3, 1, 4)
        .reshape(page_count, local_kv, 2, PAGE * HEAD)
    )

    query_heads = in_order(q_own, q_other).transpose(1, 0, 2)
    key_heads = keys.transpose(1, 0, 2)
    value_heads = values.transpose(1, 0, 2)
    link_partner = [
        (r * tp_count + t, (r ^ 2) * tp_count + (tp_count - 1 - t))
        for r in range(req_count)
        for t in range(tp_count)
    ]
    w_out_other = lax.ppermute(w_out, ("req", "tp"), link_partner)

    def attend_half(start):
        meta = block_meta(segment_ids, (start // BLOCK).astype(jnp.int32))
        attended = flash_attention(meta, query_heads, key_heads, value_heads, segment_ids, blocks)
        return attended.transpose(1, 0, 2).reshape(half_len, local_query * HEAD)

    attended_in = lax.ppermute(attend_half(other_start), "tp", swap)
    attended_own = attend_half(own_start)
    projected_out = jnp.dot(attended_own, w_out, preferred_element_type=jnp.float32) + jnp.dot(
        attended_in, w_out_other, preferred_element_type=jnp.float32
    )
    hidden_out = (hidden_in.astype(jnp.float32) + projected_out).astype(jnp.bfloat16)
    return (hidden_out, cache_rows)


def solution(mesh):
    placed = (P(("req", "tp"), None), P("req"), P("req"), P(), P(None, "tp"), P("tp", None))
    return jax.shard_map(
        shards,
        mesh=mesh,
        in_specs=placed,
        out_specs=(P(("req", "tp"), None), P("req", "tp", None, None)),
        check_vma=False,
    )
```

```python
import functools
import math

import jax
import jax.numpy as jnp
from jax import lax
from jax.experimental import pallas as pl
from jax.experimental.pallas import tpu as pltpu
from jax.sharding import PartitionSpec as P

HEAD = 96
HEADS_Q = 8
HEADS_KV = 4
PAGE = 64
REQS = 8
BLOCK = 256
KEY_BLOCK = 512


rotary_base = 100000.0
norm_eps = 1e-05
masked_score = -1e30


def positions_of(segments):
    length = segments.shape[0]
    counter = jnp.arange(length, dtype=jnp.int32)
    previous = jnp.concatenate([segments[:1] - 1, segments[:-1]])
    starts = lax.cummax(jnp.where(segments != previous, counter, 0), axis=0)
    prefix_len = jnp.sum((segments == 0).astype(jnp.int32))
    return counter - starts + jnp.where(segments > 0, prefix_len, 0)


def rotary_tables(positions, width):
    half_width = width // 2
    exponent = jnp.arange(half_width, dtype=jnp.float32) * (2.0 / width)
    inverse = jnp.power(jnp.float32(rotary_base), -exponent)
    angles = positions.astype(jnp.float32)[:, None] * inverse[None, :]
    return (jnp.cos(angles), jnp.sin(angles))


def rotate(vectors, cosine, sine_table):
    half_width = vectors.shape[-1] // 2
    front_half = vectors[..., :half_width]
    second = vectors[..., half_width:]
    cosine = cosine[:, None, :]
    sine_table = sine_table[:, None, :]
    return jnp.concatenate(
        [front_half * cosine - second * sine_table, second * cosine + front_half * sine_table],
        axis=-1,
    )


def normalize(token_rows, gain_vector):
    values = token_rows.astype(jnp.float32)
    inverse_root = lax.rsqrt(jnp.mean(values * values, axis=-1, keepdims=True) + norm_eps)
    return (values * inverse_root * gain_vector.astype(jnp.float32)).astype(jnp.bfloat16)


def flash_kernel(key_width, meta_ref, q_ref, kt_ref, v_ref, segq_ref, segk_ref, o_ref, m_sc, l_sc, acc_sc):
    step = pl.program_id(0)
    query_block = meta_ref[0] + step
    prefix_blocks = meta_ref[1]
    low_block = meta_ref[2 + query_block]
    kv_heads = kt_ref.shape[0]
    group = q_ref.shape[0] // kv_heads
    m_sc[...] = jnp.full(m_sc.shape, masked_score, jnp.float32)
    l_sc[...] = jnp.zeros(l_sc.shape, jnp.float32)
    acc_sc[...] = jnp.zeros(acc_sc.shape, jnp.float32)
    rows = query_block * BLOCK + lax.broadcasted_iota(jnp.int32, (BLOCK, 1), 0)
    query_segments = segq_ref[...]

    def body(key_block, carry):
        @pl.when((key_block < prefix_blocks) | (key_block >= low_block))
        def _():
            start = pl.multiple_of(key_block * key_width, key_width)
            key_segments = segk_ref[:, pl.ds(start, key_width)]
            cols = start + lax.broadcasted_iota(jnp.int32, (1, key_width), 1)
            allowed = (cols <= rows) & ((key_segments == query_segments) | (key_segments == 0))
            bias = jnp.where(allowed, 0.0, masked_score)
            for kv_head in range(kv_heads):
                queries = q_ref[kv_head * group : (kv_head + 1) * group].reshape(group * BLOCK, HEAD)
                scores = jnp.dot(
                    queries, kt_ref[kv_head, :, pl.ds(start, key_width)], preferred_element_type=jnp.float32
                ) * (HEAD ** (-0.5))
                scores = (scores.reshape(group, BLOCK, key_width) + bias[None]).reshape(group * BLOCK, key_width)
                m_prev = m_sc[kv_head]
                m_new = jnp.maximum(m_prev, jnp.max(scores, axis=-1, keepdims=True))
                alpha = jnp.exp(m_prev - m_new)
                weights = jnp.exp(scores - m_new)
                l_sc[kv_head] = alpha * l_sc[kv_head] + jnp.sum(weights, axis=-1, keepdims=True)
                acc_sc[kv_head] = alpha * acc_sc[kv_head] + jnp.dot(
                    weights.astype(jnp.bfloat16),
                    v_ref[kv_head, pl.ds(start, key_width), :],
                    preferred_element_type=jnp.float32,
                )
                m_sc[kv_head] = m_new
        return carry

    lax.fori_loop(0, ((query_block + 1) * BLOCK + key_width - 1) // key_width, body, 0)
    for kv_head in range(kv_heads):
        o_ref[kv_head * group : (kv_head + 1) * group] = (
            (acc_sc[kv_head] / l_sc[kv_head]).reshape(group, BLOCK, HEAD).astype(o_ref.dtype)
        )


def flash_attention(meta, queries, keys, values, segments, steps, key_width=KEY_BLOCK, interpret=False):
    query_heads, length, _ = queries.shape
    kv_heads = keys.shape[0]
    group = query_heads // kv_heads
    grid_spec = pltpu.PrefetchScalarGridSpec(
        num_scalar_prefetch=1,
        grid=(steps,),
        in_specs=[
            pl.BlockSpec((query_heads, BLOCK, HEAD), lambda i, m: (0, m[0] + i, 0)),
            pl.BlockSpec((kv_heads, HEAD, length), lambda i, m: (0, 0, 0)),
            pl.BlockSpec((kv_heads, length, HEAD), lambda i, m: (0, 0, 0)),
            pl.BlockSpec((BLOCK, 1), lambda i, m: (m[0] + i, 0)),
            pl.BlockSpec((1, length), lambda i, m: (0, 0)),
        ],
        out_specs=pl.BlockSpec((query_heads, BLOCK, HEAD), lambda i, m: (0, i, 0)),
        scratch_shapes=[
            pltpu.VMEM((kv_heads, group * BLOCK, 1), jnp.float32),
            pltpu.VMEM((kv_heads, group * BLOCK, 1), jnp.float32),
            pltpu.VMEM((kv_heads, group * BLOCK, HEAD), jnp.float32),
        ],
    )
    return pl.pallas_call(
        functools.partial(flash_kernel, key_width),
        grid_spec=grid_spec,
        out_shape=jax.ShapeDtypeStruct((query_heads, steps * BLOCK, HEAD), jnp.bfloat16),
        compiler_params=pltpu.CompilerParams(dimension_semantics=("arbitrary",)),
        interpret=interpret,
    )(meta, queries, keys.transpose(0, 2, 1), values, segments.reshape(length, 1), segments.reshape(1, length))


def block_meta(segments, base, key_width=KEY_BLOCK):
    length = segments.shape[0]
    counter = jnp.arange(length, dtype=jnp.int32)
    previous = jnp.concatenate([segments[:1] - 1, segments[:-1]])
    starts = lax.cummax(jnp.where(segments != previous, counter, 0), axis=0)
    prefix_len = jnp.sum((segments == 0).astype(jnp.int32))
    prefix_blocks = (prefix_len + key_width - 1) // key_width
    low = starts[::BLOCK] // key_width
    return jnp.concatenate([jnp.stack([base, prefix_blocks]).astype(jnp.int32), low.astype(jnp.int32)])


def project(normed, w_qkv, cosine, sine_table, local_query, local_kv):
    rows = normed.shape[0]
    query_width = local_query * HEAD
    kv_width = local_kv * HEAD
    projected = jnp.dot(normed, w_qkv, preferred_element_type=jnp.float32)
    queries = rotate(
        projected[:, :query_width].reshape(rows, local_query, HEAD), cosine, sine_table
    ).astype(jnp.bfloat16)
    keys = rotate(
        projected[:, query_width : query_width + kv_width].reshape(rows, local_kv, HEAD),
        cosine,
        sine_table,
    ).astype(jnp.bfloat16)
    values = projected[:, query_width + kv_width :].reshape(rows, local_kv, HEAD).astype(jnp.bfloat16)
    return queries, keys, values


def pages_of(keys, values):
    count = keys.shape[0] // PAGE
    local_kv = keys.shape[1]
    key_pages = keys.reshape(count, PAGE, local_kv, HEAD).transpose(0, 2, 1, 3)
    value_pages = values.reshape(count, PAGE, local_kv, HEAD).transpose(0, 2, 1, 3)
    return jnp.stack([key_pages, value_pages], axis=2).reshape(count, local_kv, 2, PAGE * HEAD)


def shards(hidden_in, segment_ids, page_owner, norm_gain, w_qkv, w_out):
    tp_count = lax.axis_size("tp")
    req_count = lax.axis_size("req")
    tp_index = lax.axis_index("tp")
    group_len = segment_ids.shape[0]
    half_len = hidden_in.shape[0]
    local_query = HEADS_Q // tp_count
    local_kv = HEADS_KV // tp_count
    swap = [(0, 1), (1, 0)]
    blocks = half_len // BLOCK
    first = tp_index == 0
    own_start = tp_index * half_len
    other_start = (1 - tp_index) * half_len
    page_count = group_len // PAGE
    positions = positions_of(segment_ids)
    cosine, sine_table = rotary_tables(positions, HEAD)

    def rows_of(array, begin):
        return lax.dynamic_slice_in_dim(array, begin, half_len, axis=0)

    def in_order(own, other):
        return jnp.where(
            first, jnp.concatenate([own, other], axis=0), jnp.concatenate([other, own], axis=0)
        )

    normed_own = normalize(hidden_in, norm_gain)
    normed_other = jnp.concatenate(
        [
            normalize(lax.ppermute(hidden_in[c * BLOCK : (c + 1) * BLOCK], "tp", swap), norm_gain)
            for c in range(blocks)
        ],
        axis=0,
    )
    q_own, k_own, v_own = project(
        normed_own, w_qkv, rows_of(cosine, own_start), rows_of(sine_table, own_start), local_query, local_kv
    )
    q_other, k_other, v_other = project(
        normed_other, w_qkv, rows_of(cosine, other_start), rows_of(sine_table, other_start), local_query, local_kv
    )
    keys = in_order(k_own, k_other)
    values = in_order(v_own, v_other)

    page_data = in_order(pages_of(k_own, v_own), pages_of(k_other, v_other))
    live_pages = segment_ids[::PAGE] != REQS + 1
    owner_ids = jnp.arange(req_count, dtype=jnp.int32)
    page_numbers = jnp.arange(page_count, dtype=jnp.int32)
    to_owner = (page_owner[None, :] == owner_ids[:, None]) & live_pages[None, :]
    send_index = jnp.argmax(to_owner, axis=1)
    has_page = jnp.any(to_owner, axis=1)
    tag = jnp.where(has_page, send_index + 1, 0).astype(jnp.bfloat16)
    payload = page_data.shape[-1]
    send_pages = jnp.concatenate(
        [
            jnp.where(
                has_page[:, None, None, None], jnp.take(page_data, send_index, axis=0), 0
            ).astype(jnp.bfloat16),
            jnp.broadcast_to(tag[:, None, None, None], (req_count, local_kv, 2, 128)),
        ],
        axis=3,
    )
    received = lax.all_to_all(send_pages, "req", split_axis=0, concat_axis=0, tiled=True)
    received_ids = received[:, 0, 0, payload].astype(jnp.int32) - 1
    from_group = received_ids[None, :] == page_numbers[:, None]
    source_group = jnp.argmax(from_group, axis=1)
    cache_rows = jnp.where(
        jnp.any(from_group, axis=1)[:, None, None, None],
        jnp.take(received, source_group, axis=0)[..., :payload],
        0,
    ).astype(jnp.bfloat16)

    query_heads = in_order(q_own, q_other).transpose(1, 0, 2)
    key_heads = keys.transpose(1, 0, 2)
    value_heads = values.transpose(1, 0, 2)
    link_partner = [
        (r * tp_count + t, (r ^ 2) * tp_count + (tp_count - 1 - t))
        for r in range(req_count)
        for t in range(tp_count)
    ]
    w_out_other = lax.ppermute(w_out, ("req", "tp"), link_partner)

    def attend_half(start):
        meta = block_meta(segment_ids, (start // BLOCK).astype(jnp.int32))
        attended = flash_attention(meta, query_heads, key_heads, value_heads, segment_ids, blocks)
        return attended.transpose(1, 0, 2).reshape(half_len, local_query * HEAD)

    attended_in = lax.ppermute(attend_half(other_start), "tp", swap)
    attended_own = attend_half(own_start)
    projected_out = jnp.dot(attended_own, w_out, preferred_element_type=jnp.float32) + jnp.dot(
        attended_in, w_out_other, preferred_element_type=jnp.float32
    )
    hidden_out = (hidden_in.astype(jnp.float32) + projected_out).astype(jnp.bfloat16)
    return (hidden_out, cache_rows)


def solution(mesh):
    placed = (P(("req", "tp"), None), P("req"), P("req"), P(), P(None, "tp"), P("tp", None))
    return jax.shard_map(
        shards,
        mesh=mesh,
        in_specs=placed,
        out_specs=(P(("req", "tp"), None), P("req", "tp", None, None)),
        check_vma=False,
    )
```

```python
import functools
import math

import jax
import jax.numpy as jnp
from jax import lax
from jax.experimental import pallas as pl
from jax.experimental.pallas import tpu as pltpu
from jax.sharding import PartitionSpec as P

HEAD = 96
HEADS_Q = 8
HEADS_KV = 4
PAGE = 64
REQS = 8
BLOCK = 256
KEY_BLOCK = 512


rotary_base = 100000.0
norm_eps = 1e-05
masked_score = -1e30


def positions_of(segments):
    length = segments.shape[0]
    counter = jnp.arange(length, dtype=jnp.int32)
    previous = jnp.concatenate([segments[:1] - 1, segments[:-1]])
    starts = lax.cummax(jnp.where(segments != previous, counter, 0), axis=0)
    prefix_len = jnp.sum((segments == 0).astype(jnp.int32))
    return counter - starts + jnp.where(segments > 0, prefix_len, 0)


def rotary_tables(positions, width):
    half_width = width // 2
    exponent = jnp.arange(half_width, dtype=jnp.float32) * (2.0 / width)
    inverse = jnp.power(jnp.float32(rotary_base), -exponent)
    angles = positions.astype(jnp.float32)[:, None] * inverse[None, :]
    return (jnp.cos(angles), jnp.sin(angles))


def rotate(vectors, cosine, sine_table):
    half_width = vectors.shape[-1] // 2
    front_half = vectors[..., :half_width]
    second = vectors[..., half_width:]
    cosine = cosine[:, None, :]
    sine_table = sine_table[:, None, :]
    return jnp.concatenate(
        [front_half * cosine - second * sine_table, second * cosine + front_half * sine_table],
        axis=-1,
    )


def normalize(token_rows, gain_vector):
    values = token_rows.astype(jnp.float32)
    inverse_root = lax.rsqrt(jnp.mean(values * values, axis=-1, keepdims=True) + norm_eps)
    return (values * inverse_root * gain_vector.astype(jnp.float32)).astype(jnp.bfloat16)


def flash_kernel(key_width, meta_ref, q_ref, kt_ref, v_ref, segq_ref, segk_ref, o_ref, m_sc, l_sc, acc_sc):
    step = pl.program_id(0)
    query_block = meta_ref[0] + step
    prefix_blocks = meta_ref[1]
    low_block = meta_ref[2 + query_block]
    kv_heads = kt_ref.shape[0]
    group = q_ref.shape[0] // kv_heads
    m_sc[...] = jnp.full(m_sc.shape, masked_score, jnp.float32)
    l_sc[...] = jnp.zeros(l_sc.shape, jnp.float32)
    acc_sc[...] = jnp.zeros(acc_sc.shape, jnp.float32)
    rows = query_block * BLOCK + lax.broadcasted_iota(jnp.int32, (BLOCK, 1), 0)
    query_segments = segq_ref[...]

    def body(key_block, carry):
        @pl.when((key_block < prefix_blocks) | (key_block >= low_block))
        def _():
            start = pl.multiple_of(key_block * key_width, key_width)
            key_segments = segk_ref[:, pl.ds(start, key_width)]
            cols = start + lax.broadcasted_iota(jnp.int32, (1, key_width), 1)
            allowed = (cols <= rows) & ((key_segments == query_segments) | (key_segments == 0))
            bias = jnp.where(allowed, 0.0, masked_score)
            for kv_head in range(kv_heads):
                queries = q_ref[kv_head * group : (kv_head + 1) * group].reshape(group * BLOCK, HEAD)
                scores = jnp.dot(
                    queries, kt_ref[kv_head, :, pl.ds(start, key_width)], preferred_element_type=jnp.float32
                ) * (HEAD ** (-0.5))
                scores = (scores.reshape(group, BLOCK, key_width) + bias[None]).reshape(group * BLOCK, key_width)
                m_prev = m_sc[kv_head]
                m_new = jnp.maximum(m_prev, jnp.max(scores, axis=-1, keepdims=True))
                alpha = jnp.exp(m_prev - m_new)
                weights = jnp.exp(scores - m_new)
                l_sc[kv_head] = alpha * l_sc[kv_head] + jnp.sum(weights, axis=-1, keepdims=True)
                acc_sc[kv_head] = alpha * acc_sc[kv_head] + jnp.dot(
                    weights.astype(jnp.bfloat16),
                    v_ref[kv_head, pl.ds(start, key_width), :],
                    preferred_element_type=jnp.float32,
                )
                m_sc[kv_head] = m_new
        return carry

    lax.fori_loop(0, ((query_block + 1) * BLOCK + key_width - 1) // key_width, body, 0)
    for kv_head in range(kv_heads):
        o_ref[kv_head * group : (kv_head + 1) * group] = (
            (acc_sc[kv_head] / l_sc[kv_head]).reshape(group, BLOCK, HEAD).astype(o_ref.dtype)
        )


def flash_attention(meta, queries, keys, values, segments, steps, key_width=KEY_BLOCK, interpret=False):
    query_heads, length, _ = queries.shape
    kv_heads = keys.shape[0]
    group = query_heads // kv_heads
    grid_spec = pltpu.PrefetchScalarGridSpec(
        num_scalar_prefetch=1,
        grid=(steps,),
        in_specs=[
            pl.BlockSpec((query_heads, BLOCK, HEAD), lambda i, m: (0, m[0] + i, 0)),
            pl.BlockSpec((kv_heads, HEAD, length), lambda i, m: (0, 0, 0)),
            pl.BlockSpec((kv_heads, length, HEAD), lambda i, m: (0, 0, 0)),
            pl.BlockSpec((BLOCK, 1), lambda i, m: (m[0] + i, 0)),
            pl.BlockSpec((1, length), lambda i, m: (0, 0)),
        ],
        out_specs=pl.BlockSpec((query_heads, BLOCK, HEAD), lambda i, m: (0, i, 0)),
        scratch_shapes=[
            pltpu.VMEM((kv_heads, group * BLOCK, 1), jnp.float32),
            pltpu.VMEM((kv_heads, group * BLOCK, 1), jnp.float32),
            pltpu.VMEM((kv_heads, group * BLOCK, HEAD), jnp.float32),
        ],
    )
    return pl.pallas_call(
        functools.partial(flash_kernel, key_width),
        grid_spec=grid_spec,
        out_shape=jax.ShapeDtypeStruct((query_heads, steps * BLOCK, HEAD), jnp.bfloat16),
        compiler_params=pltpu.CompilerParams(dimension_semantics=("arbitrary",)),
        interpret=interpret,
    )(meta, queries, keys.transpose(0, 2, 1), values, segments.reshape(length, 1), segments.reshape(1, length))


def block_meta(segments, base, key_width=KEY_BLOCK):
    length = segments.shape[0]
    counter = jnp.arange(length, dtype=jnp.int32)
    previous = jnp.concatenate([segments[:1] - 1, segments[:-1]])
    starts = lax.cummax(jnp.where(segments != previous, counter, 0), axis=0)
    prefix_len = jnp.sum((segments == 0).astype(jnp.int32))
    prefix_blocks = (prefix_len + key_width - 1) // key_width
    low = starts[::BLOCK] // key_width
    return jnp.concatenate([jnp.stack([base, prefix_blocks]).astype(jnp.int32), low.astype(jnp.int32)])


def project(normed, w_all, cosine, sine_table, local_query, local_kv):
    rows = normed.shape[0]
    rotary_heads = local_query + local_kv
    rotary_width = rotary_heads * HEAD
    kv_width = local_kv * HEAD
    projected = jnp.dot(normed, w_all, preferred_element_type=jnp.float32)
    cosine = jnp.concatenate([cosine, cosine], axis=-1)[:, None, :]
    sine_table = jnp.concatenate([sine_table, sine_table], axis=-1)[:, None, :]
    plain = projected[:, :rotary_width].reshape(rows, rotary_heads, HEAD)
    swapped = projected[:, rotary_width + kv_width :].reshape(rows, rotary_heads, HEAD)
    rotated = (plain * cosine + swapped * sine_table).astype(jnp.bfloat16)
    values = projected[:, rotary_width : rotary_width + kv_width].reshape(rows, local_kv, HEAD)
    return rotated[:, :local_query], rotated[:, local_query:], values.astype(jnp.bfloat16)


def pages_of(keys, values):
    count = keys.shape[0] // PAGE
    local_kv = keys.shape[1]
    key_pages = keys.reshape(count, PAGE, local_kv, HEAD).transpose(0, 2, 1, 3)
    value_pages = values.reshape(count, PAGE, local_kv, HEAD).transpose(0, 2, 1, 3)
    return jnp.stack([key_pages, value_pages], axis=2).reshape(count, local_kv, 2, PAGE * HEAD)


def shards(hidden_in, segment_ids, page_owner, norm_gain, w_qkv, w_out):
    tp_count = lax.axis_size("tp")
    req_count = lax.axis_size("req")
    tp_index = lax.axis_index("tp")
    group_len = segment_ids.shape[0]
    half_len = hidden_in.shape[0]
    local_query = HEADS_Q // tp_count
    local_kv = HEADS_KV // tp_count
    swap = [(0, 1), (1, 0)]
    blocks = half_len // BLOCK
    first = tp_index == 0
    own_start = tp_index * half_len
    other_start = (1 - tp_index) * half_len
    page_count = group_len // PAGE
    positions = positions_of(segment_ids)
    cosine, sine_table = rotary_tables(positions, HEAD)

    def rows_of(array, begin):
        return lax.dynamic_slice_in_dim(array, begin, half_len, axis=0)

    def in_order(own, other):
        return jnp.where(
            first, jnp.concatenate([own, other], axis=0), jnp.concatenate([other, own], axis=0)
        )

    rotary_width = (local_query + local_kv) * HEAD
    halves = w_qkv[:, :rotary_width].reshape(w_qkv.shape[0], local_query + local_kv, 2, HEAD // 2)
    w_swapped = jnp.concatenate([-halves[:, :, 1], halves[:, :, 0]], axis=2).reshape(
        w_qkv.shape[0], rotary_width
    )
    w_all = jnp.concatenate([w_qkv, w_swapped], axis=1)
    normed_own = normalize(hidden_in, norm_gain)
    normed_other = jnp.concatenate(
        [
            normalize(lax.ppermute(hidden_in[c * BLOCK : (c + 1) * BLOCK], "tp", swap), norm_gain)
            for c in range(blocks)
        ],
        axis=0,
    )
    q_own, k_own, v_own = project(
        normed_own, w_all, rows_of(cosine, own_start), rows_of(sine_table, own_start), local_query, local_kv
    )
    q_other, k_other, v_other = project(
        normed_other, w_all, rows_of(cosine, other_start), rows_of(sine_table, other_start), local_query, local_kv
    )
    keys = in_order(k_own, k_other)
    values = in_order(v_own, v_other)

    page_data = in_order(pages_of(k_own, v_own), pages_of(k_other, v_other))
    live_pages = segment_ids[::PAGE] != REQS + 1
    owner_ids = jnp.arange(req_count, dtype=jnp.int32)
    page_numbers = jnp.arange(page_count, dtype=jnp.int32)
    to_owner = (page_owner[None, :] == owner_ids[:, None]) & live_pages[None, :]
    send_index = jnp.argmax(to_owner, axis=1)
    has_page = jnp.any(to_owner, axis=1)
    tag = jnp.where(has_page, send_index + 1, 0).astype(jnp.bfloat16)
    payload = page_data.shape[-1]
    send_pages = jnp.concatenate(
        [
            jnp.where(
                has_page[:, None, None, None], jnp.take(page_data, send_index, axis=0), 0
            ).astype(jnp.bfloat16),
            jnp.broadcast_to(tag[:, None, None, None], (req_count, local_kv, 2, 128)),
        ],
        axis=3,
    )
    received = lax.all_to_all(send_pages, "req", split_axis=0, concat_axis=0, tiled=True)
    received_ids = received[:, 0, 0, payload].astype(jnp.int32) - 1
    from_group = received_ids[None, :] == page_numbers[:, None]
    source_group = jnp.argmax(from_group, axis=1)
    cache_rows = jnp.where(
        jnp.any(from_group, axis=1)[:, None, None, None],
        jnp.take(received, source_group, axis=0)[..., :payload],
        0,
    ).astype(jnp.bfloat16)

    query_heads = in_order(q_own, q_other).transpose(1, 0, 2)
    key_heads = keys.transpose(1, 0, 2)
    value_heads = values.transpose(1, 0, 2)
    link_partner = [
        (r * tp_count + t, (r ^ 2) * tp_count + (tp_count - 1 - t))
        for r in range(req_count)
        for t in range(tp_count)
    ]
    w_out_other = lax.ppermute(w_out, ("req", "tp"), link_partner)

    def attend_half(start):
        meta = block_meta(segment_ids, (start // BLOCK).astype(jnp.int32))
        attended = flash_attention(meta, query_heads, key_heads, value_heads, segment_ids, blocks)
        return attended.transpose(1, 0, 2).reshape(half_len, local_query * HEAD)

    attended_in = lax.ppermute(attend_half(other_start), "tp", swap)
    attended_own = attend_half(own_start)
    projected_out = jnp.dot(attended_own, w_out, preferred_element_type=jnp.float32) + jnp.dot(
        attended_in, w_out_other, preferred_element_type=jnp.float32
    )
    hidden_out = (hidden_in.astype(jnp.float32) + projected_out).astype(jnp.bfloat16)
    return (hidden_out, cache_rows)


def solution(mesh):
    placed = (P(("req", "tp"), None), P("req"), P("req"), P(), P(None, "tp"), P("tp", None))
    return jax.shard_map(
        shards,
        mesh=mesh,
        in_specs=placed,
        out_specs=(P(("req", "tp"), None), P("req", "tp", None, None)),
        check_vma=False,
    )
```

```python
import functools
import math

import jax
import jax.numpy as jnp
from jax import lax
from jax.experimental import pallas as pl
from jax.experimental.pallas import tpu as pltpu
from jax.sharding import PartitionSpec as P

HEAD = 96
HEADS_Q = 8
HEADS_KV = 4
PAGE = 64
REQS = 8
BLOCK = 256
KEY_BLOCK = 512


rotary_base = 100000.0
norm_eps = 1e-05
masked_score = -1e30


def positions_of(segments):
    length = segments.shape[0]
    counter = jnp.arange(length, dtype=jnp.int32)
    previous = jnp.concatenate([segments[:1] - 1, segments[:-1]])
    starts = lax.cummax(jnp.where(segments != previous, counter, 0), axis=0)
    prefix_len = jnp.sum((segments == 0).astype(jnp.int32))
    return counter - starts + jnp.where(segments > 0, prefix_len, 0)


def rotary_tables(positions, width):
    half_width = width // 2
    exponent = jnp.arange(half_width, dtype=jnp.float32) * (2.0 / width)
    inverse = jnp.power(jnp.float32(rotary_base), -exponent)
    angles = positions.astype(jnp.float32)[:, None] * inverse[None, :]
    return (jnp.cos(angles), jnp.sin(angles))


def rotate(vectors, cosine, sine_table):
    half_width = vectors.shape[-1] // 2
    front_half = vectors[..., :half_width]
    second = vectors[..., half_width:]
    cosine = cosine[:, None, :]
    sine_table = sine_table[:, None, :]
    return jnp.concatenate(
        [front_half * cosine - second * sine_table, second * cosine + front_half * sine_table],
        axis=-1,
    )


def normalize(token_rows, gain_vector):
    values = token_rows.astype(jnp.float32)
    inverse_root = lax.rsqrt(jnp.mean(values * values, axis=-1, keepdims=True) + norm_eps)
    return (values * inverse_root * gain_vector.astype(jnp.float32)).astype(jnp.bfloat16)


def flash_kernel(key_width, meta_ref, q_ref, kt_ref, v_ref, segq_ref, segk_ref, o_ref, m_sc, l_sc, acc_sc):
    step = pl.program_id(0)
    query_block = meta_ref[0] + step
    prefix_blocks = meta_ref[1]
    low_block = meta_ref[2 + query_block]
    kv_heads = kt_ref.shape[0]
    group = q_ref.shape[0] // kv_heads
    m_sc[...] = jnp.full(m_sc.shape, masked_score, jnp.float32)
    l_sc[...] = jnp.zeros(l_sc.shape, jnp.float32)
    acc_sc[...] = jnp.zeros(acc_sc.shape, jnp.float32)
    rows = query_block * BLOCK + lax.broadcasted_iota(jnp.int32, (BLOCK, 1), 0)
    query_segments = segq_ref[...]

    def body(key_block, carry):
        @pl.when((key_block < prefix_blocks) | (key_block >= low_block))
        def _():
            start = pl.multiple_of(key_block * key_width, key_width)
            key_segments = segk_ref[:, pl.ds(start, key_width)]
            cols = start + lax.broadcasted_iota(jnp.int32, (1, key_width), 1)
            allowed = (cols <= rows) & ((key_segments == query_segments) | (key_segments == 0))
            bias = jnp.where(allowed, 0.0, masked_score)
            for kv_head in range(kv_heads):
                queries = q_ref[kv_head * group : (kv_head + 1) * group].reshape(group * BLOCK, HEAD)
                scores = jnp.dot(
                    queries, kt_ref[kv_head, :, pl.ds(start, key_width)], preferred_element_type=jnp.float32
                ) * (HEAD ** (-0.5))
                scores = (scores.reshape(group, BLOCK, key_width) + bias[None]).reshape(group * BLOCK, key_width)
                m_prev = m_sc[kv_head]
                m_new = jnp.maximum(m_prev, jnp.max(scores, axis=-1, keepdims=True))
                alpha = jnp.exp(m_prev - m_new)
                weights = jnp.exp(scores - m_new)
                l_sc[kv_head] = alpha * l_sc[kv_head] + jnp.sum(weights, axis=-1, keepdims=True)
                acc_sc[kv_head] = alpha * acc_sc[kv_head] + jnp.dot(
                    weights.astype(jnp.bfloat16),
                    v_ref[kv_head, pl.ds(start, key_width), :],
                    preferred_element_type=jnp.float32,
                )
                m_sc[kv_head] = m_new
        return carry

    lax.fori_loop(0, ((query_block + 1) * BLOCK + key_width - 1) // key_width, body, 0)
    for kv_head in range(kv_heads):
        o_ref[kv_head * group : (kv_head + 1) * group] = (
            (acc_sc[kv_head] / l_sc[kv_head]).reshape(group, BLOCK, HEAD).astype(o_ref.dtype)
        )


def flash_attention(meta, queries, keys, values, segments, steps, key_width=KEY_BLOCK, interpret=False):
    query_heads, length, _ = queries.shape
    kv_heads = keys.shape[0]
    group = query_heads // kv_heads
    grid_spec = pltpu.PrefetchScalarGridSpec(
        num_scalar_prefetch=1,
        grid=(steps,),
        in_specs=[
            pl.BlockSpec((query_heads, BLOCK, HEAD), lambda i, m: (0, m[0] + i, 0)),
            pl.BlockSpec((kv_heads, HEAD, length), lambda i, m: (0, 0, 0)),
            pl.BlockSpec((kv_heads, length, HEAD), lambda i, m: (0, 0, 0)),
            pl.BlockSpec((BLOCK, 1), lambda i, m: (m[0] + i, 0)),
            pl.BlockSpec((1, length), lambda i, m: (0, 0)),
        ],
        out_specs=pl.BlockSpec((query_heads, BLOCK, HEAD), lambda i, m: (0, i, 0)),
        scratch_shapes=[
            pltpu.VMEM((kv_heads, group * BLOCK, 1), jnp.float32),
            pltpu.VMEM((kv_heads, group * BLOCK, 1), jnp.float32),
            pltpu.VMEM((kv_heads, group * BLOCK, HEAD), jnp.float32),
        ],
    )
    return pl.pallas_call(
        functools.partial(flash_kernel, key_width),
        grid_spec=grid_spec,
        out_shape=jax.ShapeDtypeStruct((query_heads, steps * BLOCK, HEAD), jnp.bfloat16),
        compiler_params=pltpu.CompilerParams(dimension_semantics=("arbitrary",)),
        interpret=interpret,
    )(meta, queries, keys.transpose(0, 2, 1), values, segments.reshape(length, 1), segments.reshape(1, length))


def block_meta(segments, base, key_width=KEY_BLOCK):
    length = segments.shape[0]
    counter = jnp.arange(length, dtype=jnp.int32)
    previous = jnp.concatenate([segments[:1] - 1, segments[:-1]])
    starts = lax.cummax(jnp.where(segments != previous, counter, 0), axis=0)
    prefix_len = jnp.sum((segments == 0).astype(jnp.int32))
    prefix_blocks = (prefix_len + key_width - 1) // key_width
    low = starts[::BLOCK] // key_width
    return jnp.concatenate([jnp.stack([base, prefix_blocks]).astype(jnp.int32), low.astype(jnp.int32)])


def send_kernel(meta_ref, own_hbm, other_hbm, tag_vmem, out_hbm, zero_vmem, sems):
    zero_vmem[...] = jnp.zeros(zero_vmem.shape, zero_vmem.dtype)
    width = own_hbm.shape[-1]
    tag_width = tag_vmem.shape[-1]

    def start(owner, carry):
        kind = meta_ref[0, owner]
        row = meta_ref[1, owner]
        target = out_hbm.at[owner, :, :, pl.ds(0, width)]

        @pl.when(kind == 1)
        def _():
            pltpu.make_async_copy(own_hbm.at[row], target, sems.at[0, owner]).start()

        @pl.when(kind == 2)
        def _():
            pltpu.make_async_copy(other_hbm.at[row], target, sems.at[0, owner]).start()

        @pl.when(kind == 0)
        def _():
            pltpu.make_async_copy(zero_vmem, target, sems.at[0, owner]).start()

        pltpu.make_async_copy(
            tag_vmem.at[owner], out_hbm.at[owner, :, :, pl.ds(width, tag_width)], sems.at[1, owner]
        ).start()
        return carry

    def wait(owner, carry):
        pltpu.make_async_copy(
            zero_vmem, out_hbm.at[owner, :, :, pl.ds(0, width)], sems.at[0, owner]
        ).wait()
        pltpu.make_async_copy(
            tag_vmem.at[owner], out_hbm.at[owner, :, :, pl.ds(width, tag_width)], sems.at[1, owner]
        ).wait()
        return carry

    lax.fori_loop(0, out_hbm.shape[0], start, 0)
    lax.fori_loop(0, out_hbm.shape[0], wait, 0)


def build_send(meta, own_pages, other_pages, tags, interpret=False):
    owners = tags.shape[0]
    shape = own_pages.shape[1:-1] + (own_pages.shape[-1] + tags.shape[-1],)
    return pl.pallas_call(
        send_kernel,
        in_specs=[
            pl.BlockSpec(memory_space=pltpu.SMEM),
            pl.BlockSpec(memory_space=pl.ANY),
            pl.BlockSpec(memory_space=pl.ANY),
            pl.BlockSpec(memory_space=pltpu.VMEM),
        ],
        out_specs=pl.BlockSpec(memory_space=pl.ANY),
        out_shape=jax.ShapeDtypeStruct((owners,) + shape, own_pages.dtype),
        scratch_shapes=[
            pltpu.VMEM(own_pages.shape[1:], own_pages.dtype),
            pltpu.SemaphoreType.DMA((2, owners)),
        ],
        interpret=interpret,
    )(meta, own_pages, other_pages, tags)


def place_kernel(source_ref, received_hbm, out_hbm, zero_vmem, sems):
    zero_vmem[...] = jnp.zeros(zero_vmem.shape, zero_vmem.dtype)
    width = out_hbm.shape[-1]

    def start(page, carry):
        source = source_ref[page]

        @pl.when(source >= 0)
        def _():
            pltpu.make_async_copy(
                received_hbm.at[jnp.maximum(source, 0), :, :, pl.ds(0, width)],
                out_hbm.at[page],
                sems.at[page],
            ).start()

        @pl.when(source < 0)
        def _():
            pltpu.make_async_copy(zero_vmem, out_hbm.at[page], sems.at[page]).start()

        return carry

    def wait(page, carry):
        pltpu.make_async_copy(zero_vmem, out_hbm.at[page], sems.at[page]).wait()
        return carry

    lax.fori_loop(0, out_hbm.shape[0], start, 0)
    lax.fori_loop(0, out_hbm.shape[0], wait, 0)


def place_pages(source, received, width, interpret=False):
    pages = source.shape[0]
    shape = received.shape[1:-1] + (width,)
    return pl.pallas_call(
        place_kernel,
        in_specs=[pl.BlockSpec(memory_space=pltpu.SMEM), pl.BlockSpec(memory_space=pl.ANY)],
        out_specs=pl.BlockSpec(memory_space=pl.ANY),
        out_shape=jax.ShapeDtypeStruct((pages,) + shape, received.dtype),
        scratch_shapes=[pltpu.VMEM(shape, received.dtype), pltpu.SemaphoreType.DMA((pages,))],
        interpret=interpret,
    )(source, received)


def project(normed, w_qkv, cosine, sine_table, local_query, local_kv):
    rows = normed.shape[0]
    query_width = local_query * HEAD
    kv_width = local_kv * HEAD
    projected = jnp.dot(normed, w_qkv, preferred_element_type=jnp.float32)
    queries = rotate(
        projected[:, :query_width].reshape(rows, local_query, HEAD), cosine, sine_table
    ).astype(jnp.bfloat16)
    keys = rotate(
        projected[:, query_width : query_width + kv_width].reshape(rows, local_kv, HEAD),
        cosine,
        sine_table,
    ).astype(jnp.bfloat16)
    values = projected[:, query_width + kv_width :].reshape(rows, local_kv, HEAD).astype(jnp.bfloat16)
    return queries, keys, values


def pages_of(keys, values):
    count = keys.shape[0] // PAGE
    local_kv = keys.shape[1]
    key_pages = keys.reshape(count, PAGE, local_kv, HEAD).transpose(0, 2, 1, 3)
    value_pages = values.reshape(count, PAGE, local_kv, HEAD).transpose(0, 2, 1, 3)
    return jnp.stack([key_pages, value_pages], axis=2).reshape(count, local_kv, 2, PAGE * HEAD)


def shards(hidden_in, segment_ids, page_owner, norm_gain, w_qkv, w_out):
    tp_count = lax.axis_size("tp")
    req_count = lax.axis_size("req")
    tp_index = lax.axis_index("tp")
    group_len = segment_ids.shape[0]
    half_len = hidden_in.shape[0]
    local_query = HEADS_Q // tp_count
    local_kv = HEADS_KV // tp_count
    swap = [(0, 1), (1, 0)]
    blocks = half_len // BLOCK
    first = tp_index == 0
    own_start = tp_index * half_len
    other_start = (1 - tp_index) * half_len
    page_count = group_len // PAGE
    positions = positions_of(segment_ids)
    cosine, sine_table = rotary_tables(positions, HEAD)

    def rows_of(array, begin):
        return lax.dynamic_slice_in_dim(array, begin, half_len, axis=0)

    def in_order(own, other):
        return jnp.where(
            first, jnp.concatenate([own, other], axis=0), jnp.concatenate([other, own], axis=0)
        )

    normed_own = normalize(hidden_in, norm_gain)
    normed_other = jnp.concatenate(
        [
            normalize(lax.ppermute(hidden_in[c * BLOCK : (c + 1) * BLOCK], "tp", swap), norm_gain)
            for c in range(blocks)
        ],
        axis=0,
    )
    q_own, k_own, v_own = project(
        normed_own, w_qkv, rows_of(cosine, own_start), rows_of(sine_table, own_start), local_query, local_kv
    )
    q_other, k_other, v_other = project(
        normed_other, w_qkv, rows_of(cosine, other_start), rows_of(sine_table, other_start), local_query, local_kv
    )
    keys = in_order(k_own, k_other)
    values = in_order(v_own, v_other)

    own_pages = pages_of(k_own, v_own)
    other_pages = pages_of(k_other, v_other)
    half_pages = own_pages.shape[0]
    live_pages = segment_ids[::PAGE] != REQS + 1
    owner_ids = jnp.arange(req_count, dtype=jnp.int32)
    page_numbers = jnp.arange(page_count, dtype=jnp.int32)
    to_owner = (page_owner[None, :] == owner_ids[:, None]) & live_pages[None, :]
    send_index = jnp.argmax(to_owner, axis=1).astype(jnp.int32)
    has_page = jnp.any(to_owner, axis=1)
    own_page0 = tp_index * half_pages
    in_own = (send_index >= own_page0) & (send_index < own_page0 + half_pages)
    kind = jnp.where(has_page, jnp.where(in_own, 1, 2), 0)
    row = jnp.clip(
        jnp.where(in_own, send_index - own_page0, send_index - (1 - tp_index) * half_pages),
        0,
        half_pages - 1,
    )
    tag = jnp.where(has_page, send_index + 1, 0).astype(jnp.bfloat16)
    payload = own_pages.shape[-1]
    send_pages = build_send(
        jnp.stack([kind, row]).astype(jnp.int32),
        own_pages,
        other_pages,
        jnp.broadcast_to(tag[:, None, None, None], (req_count, local_kv, 2, 128)),
    )
    received = lax.all_to_all(send_pages, "req", split_axis=0, concat_axis=0, tiled=True)
    received_ids = received[:, 0, 0, payload].astype(jnp.int32) - 1
    from_group = received_ids[None, :] == page_numbers[:, None]
    source_group = jnp.where(
        jnp.any(from_group, axis=1), jnp.argmax(from_group, axis=1), -1
    ).astype(jnp.int32)
    cache_rows = place_pages(source_group, received, payload)

    query_heads = in_order(q_own, q_other).transpose(1, 0, 2)
    key_heads = keys.transpose(1, 0, 2)
    value_heads = values.transpose(1, 0, 2)
    link_partner = [
        (r * tp_count + t, (r ^ 2) * tp_count + (tp_count - 1 - t))
        for r in range(req_count)
        for t in range(tp_count)
    ]
    w_out_other = lax.ppermute(w_out, ("req", "tp"), link_partner)

    def attend_half(start):
        meta = block_meta(segment_ids, (start // BLOCK).astype(jnp.int32))
        attended = flash_attention(meta, query_heads, key_heads, value_heads, segment_ids, blocks)
        return attended.transpose(1, 0, 2).reshape(half_len, local_query * HEAD)

    attended_in = lax.ppermute(attend_half(other_start), "tp", swap)
    attended_own = attend_half(own_start)
    projected_out = jnp.dot(attended_own, w_out, preferred_element_type=jnp.float32) + jnp.dot(
        attended_in, w_out_other, preferred_element_type=jnp.float32
    )
    hidden_out = (hidden_in.astype(jnp.float32) + projected_out).astype(jnp.bfloat16)
    return (hidden_out, cache_rows)


def solution(mesh):
    placed = (P(("req", "tp"), None), P("req"), P("req"), P(), P(None, "tp"), P("tp", None))
    return jax.shard_map(
        shards,
        mesh=mesh,
        in_specs=placed,
        out_specs=(P(("req", "tp"), None), P("req", "tp", None, None)),
        check_vma=False,
    )
```

```python
import functools
import math

import jax
import jax.numpy as jnp
from jax import lax
from jax.experimental import pallas as pl
from jax.experimental.pallas import tpu as pltpu
from jax.sharding import PartitionSpec as P

HEAD = 96
HEADS_Q = 8
HEADS_KV = 4
PAGE = 64
REQS = 8
BLOCK = 256
KEY_BLOCK = 512


rotary_base = 100000.0
norm_eps = 1e-05
masked_score = -1e30


def positions_of(segments):
    length = segments.shape[0]
    counter = jnp.arange(length, dtype=jnp.int32)
    previous = jnp.concatenate([segments[:1] - 1, segments[:-1]])
    starts = lax.cummax(jnp.where(segments != previous, counter, 0), axis=0)
    prefix_len = jnp.sum((segments == 0).astype(jnp.int32))
    return counter - starts + jnp.where(segments > 0, prefix_len, 0)


def rotary_tables(positions, width):
    half_width = width // 2
    exponent = jnp.arange(half_width, dtype=jnp.float32) * (2.0 / width)
    inverse = jnp.power(jnp.float32(rotary_base), -exponent)
    angles = positions.astype(jnp.float32)[:, None] * inverse[None, :]
    return (jnp.cos(angles), jnp.sin(angles))


def rotate(vectors, cosine, sine_table):
    half_width = vectors.shape[-1] // 2
    front_half = vectors[..., :half_width]
    second = vectors[..., half_width:]
    cosine = cosine[:, None, :]
    sine_table = sine_table[:, None, :]
    return jnp.concatenate(
        [front_half * cosine - second * sine_table, second * cosine + front_half * sine_table],
        axis=-1,
    )


def normalize(token_rows, gain_vector):
    values = token_rows.astype(jnp.float32)
    inverse_root = lax.rsqrt(jnp.mean(values * values, axis=-1, keepdims=True) + norm_eps)
    return (values * inverse_root * gain_vector.astype(jnp.float32)).astype(jnp.bfloat16)


def flash_kernel(key_width, meta_ref, q_ref, kt_ref, v_ref, segq_ref, segk_ref, o_ref, m_sc, l_sc, acc_sc):
    step = pl.program_id(0)
    query_block = meta_ref[0] + step
    prefix_blocks = meta_ref[1]
    low_block = meta_ref[2 + query_block]
    kv_heads = kt_ref.shape[0]
    group = q_ref.shape[0] // kv_heads
    m_sc[...] = jnp.full(m_sc.shape, masked_score, jnp.float32)
    l_sc[...] = jnp.zeros(l_sc.shape, jnp.float32)
    acc_sc[...] = jnp.zeros(acc_sc.shape, jnp.float32)
    rows = query_block * BLOCK + lax.broadcasted_iota(jnp.int32, (BLOCK, 1), 0)
    query_segments = segq_ref[...]

    def body(key_block, carry):
        @pl.when((key_block < prefix_blocks) | (key_block >= low_block))
        def _():
            start = pl.multiple_of(key_block * key_width, key_width)
            key_segments = segk_ref[:, pl.ds(start, key_width)]
            cols = start + lax.broadcasted_iota(jnp.int32, (1, key_width), 1)
            allowed = (cols <= rows) & ((key_segments == query_segments) | (key_segments == 0))
            bias = jnp.where(allowed, 0.0, masked_score)
            for kv_head in range(kv_heads):
                queries = q_ref[kv_head * group : (kv_head + 1) * group].reshape(group * BLOCK, HEAD)
                scores = jnp.dot(
                    queries, kt_ref[kv_head, :, pl.ds(start, key_width)], preferred_element_type=jnp.float32
                ) * (HEAD ** (-0.5))
                scores = (scores.reshape(group, BLOCK, key_width) + bias[None]).reshape(group * BLOCK, key_width)
                m_prev = m_sc[kv_head]
                m_new = jnp.maximum(m_prev, jnp.max(scores, axis=-1, keepdims=True))
                alpha = jnp.exp(m_prev - m_new)
                weights = jnp.exp(scores - m_new)
                l_sc[kv_head] = alpha * l_sc[kv_head] + jnp.sum(weights, axis=-1, keepdims=True)
                acc_sc[kv_head] = alpha * acc_sc[kv_head] + jnp.dot(
                    weights.astype(jnp.bfloat16),
                    v_ref[kv_head, pl.ds(start, key_width), :],
                    preferred_element_type=jnp.float32,
                )
                m_sc[kv_head] = m_new
        return carry

    lax.fori_loop(0, ((query_block + 1) * BLOCK + key_width - 1) // key_width, body, 0)
    for kv_head in range(kv_heads):
        o_ref[kv_head * group : (kv_head + 1) * group] = (
            (acc_sc[kv_head] / l_sc[kv_head]).reshape(group, BLOCK, HEAD).astype(o_ref.dtype)
        )


def flash_attention(meta, queries, keys, values, segments, steps, key_width=KEY_BLOCK, interpret=False):
    query_heads, length, _ = queries.shape
    kv_heads = keys.shape[0]
    group = query_heads // kv_heads
    grid_spec = pltpu.PrefetchScalarGridSpec(
        num_scalar_prefetch=1,
        grid=(steps,),
        in_specs=[
            pl.BlockSpec((query_heads, BLOCK, HEAD), lambda i, m: (0, m[0] + i, 0)),
            pl.BlockSpec((kv_heads, HEAD, length), lambda i, m: (0, 0, 0)),
            pl.BlockSpec((kv_heads, length, HEAD), lambda i, m: (0, 0, 0)),
            pl.BlockSpec((BLOCK, 1), lambda i, m: (m[0] + i, 0)),
            pl.BlockSpec((1, length), lambda i, m: (0, 0)),
        ],
        out_specs=pl.BlockSpec((query_heads, BLOCK, HEAD), lambda i, m: (0, i, 0)),
        scratch_shapes=[
            pltpu.VMEM((kv_heads, group * BLOCK, 1), jnp.float32),
            pltpu.VMEM((kv_heads, group * BLOCK, 1), jnp.float32),
            pltpu.VMEM((kv_heads, group * BLOCK, HEAD), jnp.float32),
        ],
    )
    return pl.pallas_call(
        functools.partial(flash_kernel, key_width),
        grid_spec=grid_spec,
        out_shape=jax.ShapeDtypeStruct((query_heads, steps * BLOCK, HEAD), jnp.bfloat16),
        compiler_params=pltpu.CompilerParams(dimension_semantics=("arbitrary",)),
        interpret=interpret,
    )(meta, queries, keys.transpose(0, 2, 1), values, segments.reshape(length, 1), segments.reshape(1, length))


def block_meta(segments, base, key_width=KEY_BLOCK):
    length = segments.shape[0]
    counter = jnp.arange(length, dtype=jnp.int32)
    previous = jnp.concatenate([segments[:1] - 1, segments[:-1]])
    starts = lax.cummax(jnp.where(segments != previous, counter, 0), axis=0)
    prefix_len = jnp.sum((segments == 0).astype(jnp.int32))
    prefix_blocks = (prefix_len + key_width - 1) // key_width
    low = starts[::BLOCK] // key_width
    return jnp.concatenate([jnp.stack([base, prefix_blocks]).astype(jnp.int32), low.astype(jnp.int32)])


def project(normed, w_qkv, cosine, sine_table, local_query, local_kv):
    rows = normed.shape[0]
    query_width = local_query * HEAD
    kv_width = local_kv * HEAD
    projected = jnp.dot(normed, w_qkv, preferred_element_type=jnp.float32)
    queries = rotate(
        projected[:, :query_width].reshape(rows, local_query, HEAD), cosine, sine_table
    ).astype(jnp.bfloat16)
    keys = rotate(
        projected[:, query_width : query_width + kv_width].reshape(rows, local_kv, HEAD),
        cosine,
        sine_table,
    ).astype(jnp.bfloat16)
    values = projected[:, query_width + kv_width :].reshape(rows, local_kv, HEAD).astype(jnp.bfloat16)
    return queries, keys, values


def pages_of(keys, values):
    count = keys.shape[0] // PAGE
    local_kv = keys.shape[1]
    key_pages = keys.reshape(count, PAGE, local_kv, HEAD).transpose(0, 2, 1, 3)
    value_pages = values.reshape(count, PAGE, local_kv, HEAD).transpose(0, 2, 1, 3)
    return jnp.stack([key_pages, value_pages], axis=2).reshape(count, local_kv, 2, PAGE * HEAD)


def shards(hidden_in, segment_ids, page_owner, norm_gain, w_qkv, w_out):
    tp_count = lax.axis_size("tp")
    req_count = lax.axis_size("req")
    tp_index = lax.axis_index("tp")
    group_len = segment_ids.shape[0]
    half_len = hidden_in.shape[0]
    local_query = HEADS_Q // tp_count
    local_kv = HEADS_KV // tp_count
    swap = [(0, 1), (1, 0)]
    blocks = half_len // BLOCK
    first = tp_index == 0
    own_start = tp_index * half_len
    other_start = (1 - tp_index) * half_len
    page_count = group_len // PAGE
    positions = positions_of(segment_ids)
    cosine, sine_table = rotary_tables(positions, HEAD)

    def rows_of(array, begin):
        return lax.dynamic_slice_in_dim(array, begin, half_len, axis=0)

    def in_order(own, other):
        return jnp.where(
            first, jnp.concatenate([own, other], axis=0), jnp.concatenate([other, own], axis=0)
        )

    normed_own = normalize(hidden_in, norm_gain)
    normed_other = jnp.concatenate(
        [
            normalize(lax.ppermute(hidden_in[c * BLOCK : (c + 1) * BLOCK], "tp", swap), norm_gain)
            for c in range(blocks)
        ],
        axis=0,
    )
    q_own, k_own, v_own = project(
        normed_own, w_qkv, rows_of(cosine, own_start), rows_of(sine_table, own_start), local_query, local_kv
    )
    q_other, k_other, v_other = project(
        normed_other, w_qkv, rows_of(cosine, other_start), rows_of(sine_table, other_start), local_query, local_kv
    )
    keys = in_order(k_own, k_other)
    values = in_order(v_own, v_other)

    page_data = pages_of(keys, values)
    live_pages = segment_ids[::PAGE] != REQS + 1
    owner_ids = jnp.arange(req_count, dtype=jnp.int32)
    page_numbers = jnp.arange(page_count, dtype=jnp.int32)
    to_owner = (page_owner[None, :] == owner_ids[:, None]) & live_pages[None, :]
    send_index = jnp.where(jnp.any(to_owner, axis=1), jnp.argmax(to_owner, axis=1), page_count)
    payload = page_data.shape[-1]
    tag_block = jnp.broadcast_to(
        (page_numbers + 1).astype(jnp.bfloat16)[:, None, None, None], (page_count, local_kv, 2, 128)
    )
    source_pages = jnp.concatenate(
        [
            jnp.concatenate([page_data, tag_block], axis=3),
            jnp.zeros((1, local_kv, 2, payload + 128), jnp.bfloat16),
        ],
        axis=0,
    )
    send_pages = jnp.take(source_pages, send_index, axis=0)
    received = lax.all_to_all(send_pages, "req", split_axis=0, concat_axis=0, tiled=True)
    received_ids = received[:, 0, 0, payload].astype(jnp.int32) - 1
    from_group = received_ids[None, :] == page_numbers[:, None]
    source_group = jnp.argmax(from_group, axis=1)
    cache_rows = jnp.where(
        jnp.any(from_group, axis=1)[:, None, None, None],
        jnp.take(received, source_group, axis=0)[..., :payload],
        0,
    ).astype(jnp.bfloat16)

    query_heads = in_order(q_own, q_other).transpose(1, 0, 2)
    key_heads = keys.transpose(1, 0, 2)
    value_heads = values.transpose(1, 0, 2)
    link_partner = [
        (r * tp_count + t, (r ^ 2) * tp_count + (tp_count - 1 - t))
        for r in range(req_count)
        for t in range(tp_count)
    ]
    w_out_other = lax.ppermute(w_out, ("req", "tp"), link_partner)

    def attend_half(start):
        meta = block_meta(segment_ids, (start // BLOCK).astype(jnp.int32))
        attended = flash_attention(meta, query_heads, key_heads, value_heads, segment_ids, blocks)
        return attended.transpose(1, 0, 2).reshape(half_len, local_query * HEAD)

    attended_in = lax.ppermute(attend_half(other_start), "tp", swap)
    attended_own = attend_half(own_start)
    projected_out = jnp.dot(attended_own, w_out, preferred_element_type=jnp.float32) + jnp.dot(
        attended_in, w_out_other, preferred_element_type=jnp.float32
    )
    hidden_out = (hidden_in.astype(jnp.float32) + projected_out).astype(jnp.bfloat16)
    return (hidden_out, cache_rows)


def solution(mesh):
    placed = (P(("req", "tp"), None), P("req"), P("req"), P(), P(None, "tp"), P("tp", None))
    return jax.shard_map(
        shards,
        mesh=mesh,
        in_specs=placed,
        out_specs=(P(("req", "tp"), None), P("req", "tp", None, None)),
        check_vma=False,
    )
```

```python
import functools
import math

import jax
import jax.numpy as jnp
from jax import lax
from jax.experimental import pallas as pl
from jax.experimental.pallas import tpu as pltpu
from jax.sharding import PartitionSpec as P

HEAD = 96
HEADS_Q = 8
HEADS_KV = 4
PAGE = 64
REQS = 8
BLOCK = 256
KEY_BLOCK = 512


rotary_base = 100000.0
norm_eps = 1e-05
masked_score = -1e30


def positions_of(segments):
    length = segments.shape[0]
    counter = jnp.arange(length, dtype=jnp.int32)
    previous = jnp.concatenate([segments[:1] - 1, segments[:-1]])
    starts = lax.cummax(jnp.where(segments != previous, counter, 0), axis=0)
    prefix_len = jnp.sum((segments == 0).astype(jnp.int32))
    return counter - starts + jnp.where(segments > 0, prefix_len, 0)


def rotary_tables(positions, width):
    half_width = width // 2
    exponent = jnp.arange(half_width, dtype=jnp.float32) * (2.0 / width)
    inverse = jnp.power(jnp.float32(rotary_base), -exponent)
    angles = positions.astype(jnp.float32)[:, None] * inverse[None, :]
    return (jnp.cos(angles), jnp.sin(angles))


def rotate(vectors, cosine, sine_table):
    half_width = vectors.shape[-1] // 2
    front_half = vectors[..., :half_width]
    second = vectors[..., half_width:]
    cosine = cosine[:, None, :]
    sine_table = sine_table[:, None, :]
    return jnp.concatenate(
        [front_half * cosine - second * sine_table, second * cosine + front_half * sine_table],
        axis=-1,
    )


def normalize(token_rows, gain_vector):
    values = token_rows.astype(jnp.float32)
    inverse_root = lax.rsqrt(jnp.mean(values * values, axis=-1, keepdims=True) + norm_eps)
    return (values * inverse_root * gain_vector.astype(jnp.float32)).astype(jnp.bfloat16)


def flash_kernel(key_width, meta_ref, q_ref, kt_ref, v_ref, segq_ref, segk_ref, o_ref, m_sc, l_sc, acc_sc):
    step = pl.program_id(0)
    query_block = meta_ref[0] + step
    prefix_blocks = meta_ref[1]
    low_block = meta_ref[2 + query_block]
    kv_heads = kt_ref.shape[0]
    group = q_ref.shape[0] // kv_heads
    m_sc[...] = jnp.full(m_sc.shape, masked_score, jnp.float32)
    l_sc[...] = jnp.zeros(l_sc.shape, jnp.float32)
    acc_sc[...] = jnp.zeros(acc_sc.shape, jnp.float32)
    rows = query_block * BLOCK + lax.broadcasted_iota(jnp.int32, (BLOCK, 1), 0)
    query_segments = segq_ref[...]

    def body(key_block, carry):
        @pl.when((key_block < prefix_blocks) | (key_block >= low_block))
        def _():
            start = pl.multiple_of(key_block * key_width, key_width)
            key_segments = segk_ref[:, pl.ds(start, key_width)]
            cols = start + lax.broadcasted_iota(jnp.int32, (1, key_width), 1)
            allowed = (cols <= rows) & ((key_segments == query_segments) | (key_segments == 0))
            bias = jnp.where(allowed, 0.0, masked_score)
            for kv_head in range(kv_heads):
                queries = q_ref[kv_head * group : (kv_head + 1) * group].reshape(group * BLOCK, HEAD)
                scores = jnp.dot(
                    queries, kt_ref[kv_head, :, pl.ds(start, key_width)], preferred_element_type=jnp.float32
                ) * (HEAD ** (-0.5))
                scores = (scores.reshape(group, BLOCK, key_width) + bias[None]).reshape(group * BLOCK, key_width)
                m_prev = m_sc[kv_head]
                m_new = jnp.maximum(m_prev, jnp.max(scores, axis=-1, keepdims=True))
                alpha = jnp.exp(m_prev - m_new)
                weights = jnp.exp(scores - m_new)
                l_sc[kv_head] = alpha * l_sc[kv_head] + jnp.sum(weights, axis=-1, keepdims=True)
                acc_sc[kv_head] = alpha * acc_sc[kv_head] + jnp.dot(
                    weights.astype(jnp.bfloat16),
                    v_ref[kv_head, pl.ds(start, key_width), :],
                    preferred_element_type=jnp.float32,
                )
                m_sc[kv_head] = m_new
        return carry

    lax.fori_loop(0, ((query_block + 1) * BLOCK + key_width - 1) // key_width, body, 0)
    for kv_head in range(kv_heads):
        o_ref[kv_head * group : (kv_head + 1) * group] = (
            (acc_sc[kv_head] / l_sc[kv_head]).reshape(group, BLOCK, HEAD).astype(o_ref.dtype)
        )


def flash_attention(meta, queries, keys, values, segments, steps, key_width=KEY_BLOCK, interpret=False):
    query_heads, length, _ = queries.shape
    kv_heads = keys.shape[0]
    group = query_heads // kv_heads
    grid_spec = pltpu.PrefetchScalarGridSpec(
        num_scalar_prefetch=1,
        grid=(steps,),
        in_specs=[
            pl.BlockSpec((query_heads, BLOCK, HEAD), lambda i, m: (0, m[0] + i, 0)),
            pl.BlockSpec((kv_heads, HEAD, length), lambda i, m: (0, 0, 0)),
            pl.BlockSpec((kv_heads, length, HEAD), lambda i, m: (0, 0, 0)),
            pl.BlockSpec((BLOCK, 1), lambda i, m: (m[0] + i, 0)),
            pl.BlockSpec((1, length), lambda i, m: (0, 0)),
        ],
        out_specs=pl.BlockSpec((query_heads, BLOCK, HEAD), lambda i, m: (0, i, 0)),
        scratch_shapes=[
            pltpu.VMEM((kv_heads, group * BLOCK, 1), jnp.float32),
            pltpu.VMEM((kv_heads, group * BLOCK, 1), jnp.float32),
            pltpu.VMEM((kv_heads, group * BLOCK, HEAD), jnp.float32),
        ],
    )
    return pl.pallas_call(
        functools.partial(flash_kernel, key_width),
        grid_spec=grid_spec,
        out_shape=jax.ShapeDtypeStruct((query_heads, steps * BLOCK, HEAD), jnp.bfloat16),
        compiler_params=pltpu.CompilerParams(dimension_semantics=("arbitrary",)),
        interpret=interpret,
    )(meta, queries, keys.transpose(0, 2, 1), values, segments.reshape(length, 1), segments.reshape(1, length))


def block_meta(segments, base, key_width=KEY_BLOCK):
    length = segments.shape[0]
    counter = jnp.arange(length, dtype=jnp.int32)
    previous = jnp.concatenate([segments[:1] - 1, segments[:-1]])
    starts = lax.cummax(jnp.where(segments != previous, counter, 0), axis=0)
    prefix_len = jnp.sum((segments == 0).astype(jnp.int32))
    prefix_blocks = (prefix_len + key_width - 1) // key_width
    low = starts[::BLOCK] // key_width
    return jnp.concatenate([jnp.stack([base, prefix_blocks]).astype(jnp.int32), low.astype(jnp.int32)])


def project(normed, w_qkv, cosine, sine_table, local_query, local_kv):
    rows = normed.shape[0]
    query_width = local_query * HEAD
    kv_width = local_kv * HEAD
    projected = jnp.dot(normed, w_qkv, preferred_element_type=jnp.float32)
    queries = rotate(
        projected[:, :query_width].reshape(rows, local_query, HEAD), cosine, sine_table
    ).astype(jnp.bfloat16)
    keys = rotate(
        projected[:, query_width : query_width + kv_width].reshape(rows, local_kv, HEAD),
        cosine,
        sine_table,
    ).astype(jnp.bfloat16)
    values = projected[:, query_width + kv_width :].reshape(rows, local_kv, HEAD).astype(jnp.bfloat16)
    return queries, keys, values


def pages_of(keys, values):
    count = keys.shape[0] // PAGE
    local_kv = keys.shape[1]
    key_pages = keys.reshape(count, PAGE, local_kv, HEAD).transpose(0, 2, 1, 3)
    value_pages = values.reshape(count, PAGE, local_kv, HEAD).transpose(0, 2, 1, 3)
    return jnp.stack([key_pages, value_pages], axis=2).reshape(count, local_kv, 2, PAGE * HEAD)


def shards(hidden_in, segment_ids, page_owner, norm_gain, w_qkv, w_out):
    tp_count = lax.axis_size("tp")
    req_count = lax.axis_size("req")
    tp_index = lax.axis_index("tp")
    group_len = segment_ids.shape[0]
    half_len = hidden_in.shape[0]
    local_query = HEADS_Q // tp_count
    local_kv = HEADS_KV // tp_count
    swap = [(0, 1), (1, 0)]
    blocks = half_len // BLOCK
    first = tp_index == 0
    own_start = tp_index * half_len
    other_start = (1 - tp_index) * half_len
    page_count = group_len // PAGE
    positions = positions_of(segment_ids)
    cosine, sine_table = rotary_tables(positions, HEAD)

    def rows_of(array, begin):
        return lax.dynamic_slice_in_dim(array, begin, half_len, axis=0)

    def in_order(own, other, axis=0):
        shape = list(own.shape)
        shape[axis] *= 2
        merged = jnp.zeros(shape, own.dtype)
        merged = lax.dynamic_update_slice_in_dim(merged, own, own_start, axis=axis)
        return lax.dynamic_update_slice_in_dim(merged, other, other_start, axis=axis)

    normed_own = normalize(hidden_in, norm_gain)
    normed_other = jnp.concatenate(
        [
            normalize(lax.ppermute(hidden_in[c * BLOCK : (c + 1) * BLOCK], "tp", swap), norm_gain)
            for c in range(blocks)
        ],
        axis=0,
    )
    q_own, k_own, v_own = project(
        normed_own, w_qkv, rows_of(cosine, own_start), rows_of(sine_table, own_start), local_query, local_kv
    )
    q_other, k_other, v_other = project(
        normed_other, w_qkv, rows_of(cosine, other_start), rows_of(sine_table, other_start), local_query, local_kv
    )
    keys = in_order(k_own, k_other)
    values = in_order(v_own, v_other)

    page_data = pages_of(keys, values)
    live_pages = segment_ids[::PAGE] != REQS + 1
    owner_ids = jnp.arange(req_count, dtype=jnp.int32)
    page_numbers = jnp.arange(page_count, dtype=jnp.int32)
    to_owner = (page_owner[None, :] == owner_ids[:, None]) & live_pages[None, :]
    send_index = jnp.where(jnp.any(to_owner, axis=1), jnp.argmax(to_owner, axis=1), page_count)
    payload = page_data.shape[-1]
    tag_block = jnp.broadcast_to(
        (page_numbers + 1).astype(jnp.bfloat16)[:, None, None, None], (page_count, local_kv, 2, 128)
    )
    source_pages = jnp.concatenate(
        [
            jnp.concatenate([page_data, tag_block], axis=3),
            jnp.zeros((1, local_kv, 2, payload + 128), jnp.bfloat16),
        ],
        axis=0,
    )
    send_pages = jnp.take(source_pages, send_index, axis=0)
    received = lax.all_to_all(send_pages, "req", split_axis=0, concat_axis=0, tiled=True)
    received_ids = received[:, 0, 0, payload].astype(jnp.int32) - 1
    from_group = received_ids[None, :] == page_numbers[:, None]
    source_group = jnp.argmax(from_group, axis=1)
    cache_rows = jnp.where(
        jnp.any(from_group, axis=1)[:, None, None, None],
        jnp.take(received, source_group, axis=0)[..., :payload],
        0,
    ).astype(jnp.bfloat16)

    query_heads = in_order(q_own.transpose(1, 0, 2), q_other.transpose(1, 0, 2), axis=1)
    key_heads = in_order(k_own.transpose(1, 0, 2), k_other.transpose(1, 0, 2), axis=1)
    value_heads = in_order(v_own.transpose(1, 0, 2), v_other.transpose(1, 0, 2), axis=1)
    link_partner = [
        (r * tp_count + t, (r ^ 2) * tp_count + (tp_count - 1 - t))
        for r in range(req_count)
        for t in range(tp_count)
    ]
    w_out_other = lax.ppermute(w_out, ("req", "tp"), link_partner)

    def attend_half(start):
        meta = block_meta(segment_ids, (start // BLOCK).astype(jnp.int32))
        attended = flash_attention(meta, query_heads, key_heads, value_heads, segment_ids, blocks)
        return attended.transpose(1, 0, 2).reshape(half_len, local_query * HEAD)

    attended_in = lax.ppermute(attend_half(other_start), "tp", swap)
    attended_own = attend_half(own_start)
    projected_out = jnp.dot(attended_own, w_out, preferred_element_type=jnp.float32) + jnp.dot(
        attended_in, w_out_other, preferred_element_type=jnp.float32
    )
    hidden_out = (hidden_in.astype(jnp.float32) + projected_out).astype(jnp.bfloat16)
    return (hidden_out, cache_rows)


def solution(mesh):
    placed = (P(("req", "tp"), None), P("req"), P("req"), P(), P(None, "tp"), P("tp", None))
    return jax.shard_map(
        shards,
        mesh=mesh,
        in_specs=placed,
        out_specs=(P(("req", "tp"), None), P("req", "tp", None, None)),
        check_vma=False,
    )
```

```python
import functools
import math

import jax
import jax.numpy as jnp
from jax import lax
from jax.experimental import pallas as pl
from jax.experimental.pallas import tpu as pltpu
from jax.sharding import PartitionSpec as P

HEAD = 96
HEADS_Q = 8
HEADS_KV = 4
PAGE = 64
REQS = 8
BLOCK = 256
KEY_BLOCK = 512


rotary_base = 100000.0
norm_eps = 1e-05
masked_score = -1e30


def positions_of(segments):
    length = segments.shape[0]
    counter = jnp.arange(length, dtype=jnp.int32)
    previous = jnp.concatenate([segments[:1] - 1, segments[:-1]])
    starts = lax.cummax(jnp.where(segments != previous, counter, 0), axis=0)
    prefix_len = jnp.sum((segments == 0).astype(jnp.int32))
    return counter - starts + jnp.where(segments > 0, prefix_len, 0)


def rotary_tables(positions, width):
    half_width = width // 2
    exponent = jnp.arange(half_width, dtype=jnp.float32) * (2.0 / width)
    inverse = jnp.power(jnp.float32(rotary_base), -exponent)
    angles = positions.astype(jnp.float32)[:, None] * inverse[None, :]
    return (jnp.cos(angles), jnp.sin(angles))


def rotate(vectors, cosine, sine_table):
    half_width = vectors.shape[-1] // 2
    front_half = vectors[..., :half_width]
    second = vectors[..., half_width:]
    cosine = cosine[:, None, :]
    sine_table = sine_table[:, None, :]
    return jnp.concatenate(
        [front_half * cosine - second * sine_table, second * cosine + front_half * sine_table],
        axis=-1,
    )


def normalize(token_rows, gain_vector):
    values = token_rows.astype(jnp.float32)
    inverse_root = lax.rsqrt(jnp.mean(values * values, axis=-1, keepdims=True) + norm_eps)
    return (values * inverse_root * gain_vector.astype(jnp.float32)).astype(jnp.bfloat16)


def flash_kernel(key_width, meta_ref, q_ref, kt_ref, v_ref, segq_ref, segk_ref, o_ref, m_sc, l_sc, acc_sc):
    step = pl.program_id(0)
    query_block = meta_ref[0] + step
    prefix_blocks = meta_ref[1]
    low_block = meta_ref[2 + query_block]
    kv_heads = kt_ref.shape[0]
    group = q_ref.shape[0] // kv_heads
    m_sc[...] = jnp.full(m_sc.shape, masked_score, jnp.float32)
    l_sc[...] = jnp.zeros(l_sc.shape, jnp.float32)
    acc_sc[...] = jnp.zeros(acc_sc.shape, jnp.float32)
    rows = query_block * BLOCK + lax.broadcasted_iota(jnp.int32, (BLOCK, 1), 0)
    query_segments = segq_ref[...]

    def body(key_block, carry):
        @pl.when((key_block < prefix_blocks) | (key_block >= low_block))
        def _():
            start = pl.multiple_of(key_block * key_width, key_width)
            key_segments = segk_ref[:, pl.ds(start, key_width)]
            cols = start + lax.broadcasted_iota(jnp.int32, (1, key_width), 1)
            allowed = (cols <= rows) & ((key_segments == query_segments) | (key_segments == 0))
            bias = jnp.where(allowed, 0.0, masked_score)
            for kv_head in range(kv_heads):
                queries = q_ref[kv_head * group : (kv_head + 1) * group].reshape(group * BLOCK, HEAD)
                scores = jnp.dot(
                    queries, kt_ref[kv_head, :, pl.ds(start, key_width)], preferred_element_type=jnp.float32
                ) * (HEAD ** (-0.5))
                scores = (scores.reshape(group, BLOCK, key_width) + bias[None]).reshape(group * BLOCK, key_width)
                m_prev = m_sc[kv_head]
                m_new = jnp.maximum(m_prev, jnp.max(scores, axis=-1, keepdims=True))
                alpha = jnp.exp(m_prev - m_new)
                weights = jnp.exp(scores - m_new)
                l_sc[kv_head] = alpha * l_sc[kv_head] + jnp.sum(weights, axis=-1, keepdims=True)
                acc_sc[kv_head] = alpha * acc_sc[kv_head] + jnp.dot(
                    weights.astype(jnp.bfloat16),
                    v_ref[kv_head, pl.ds(start, key_width), :],
                    preferred_element_type=jnp.float32,
                )
                m_sc[kv_head] = m_new
        return carry

    lax.fori_loop(0, ((query_block + 1) * BLOCK + key_width - 1) // key_width, body, 0)
    for kv_head in range(kv_heads):
        o_ref[kv_head * group : (kv_head + 1) * group] = (
            (acc_sc[kv_head] / l_sc[kv_head]).reshape(group, BLOCK, HEAD).astype(o_ref.dtype)
        )


def flash_attention(meta, queries, keys, values, segments, steps, key_width=KEY_BLOCK, interpret=False):
    query_heads, length, _ = queries.shape
    kv_heads = keys.shape[0]
    group = query_heads // kv_heads
    grid_spec = pltpu.PrefetchScalarGridSpec(
        num_scalar_prefetch=1,
        grid=(steps,),
        in_specs=[
            pl.BlockSpec((query_heads, BLOCK, HEAD), lambda i, m: (0, m[0] + i, 0)),
            pl.BlockSpec((kv_heads, HEAD, length), lambda i, m: (0, 0, 0)),
            pl.BlockSpec((kv_heads, length, HEAD), lambda i, m: (0, 0, 0)),
            pl.BlockSpec((BLOCK, 1), lambda i, m: (m[0] + i, 0)),
            pl.BlockSpec((1, length), lambda i, m: (0, 0)),
        ],
        out_specs=pl.BlockSpec((query_heads, BLOCK, HEAD), lambda i, m: (0, i, 0)),
        scratch_shapes=[
            pltpu.VMEM((kv_heads, group * BLOCK, 1), jnp.float32),
            pltpu.VMEM((kv_heads, group * BLOCK, 1), jnp.float32),
            pltpu.VMEM((kv_heads, group * BLOCK, HEAD), jnp.float32),
        ],
    )
    return pl.pallas_call(
        functools.partial(flash_kernel, key_width),
        grid_spec=grid_spec,
        out_shape=jax.ShapeDtypeStruct((query_heads, steps * BLOCK, HEAD), jnp.bfloat16),
        compiler_params=pltpu.CompilerParams(dimension_semantics=("arbitrary",)),
        interpret=interpret,
    )(meta, queries, keys.transpose(0, 2, 1), values, segments.reshape(length, 1), segments.reshape(1, length))


def block_meta(segments, base, key_width=KEY_BLOCK):
    length = segments.shape[0]
    counter = jnp.arange(length, dtype=jnp.int32)
    previous = jnp.concatenate([segments[:1] - 1, segments[:-1]])
    starts = lax.cummax(jnp.where(segments != previous, counter, 0), axis=0)
    prefix_len = jnp.sum((segments == 0).astype(jnp.int32))
    prefix_blocks = (prefix_len + key_width - 1) // key_width
    low = starts[::BLOCK] // key_width
    return jnp.concatenate([jnp.stack([base, prefix_blocks]).astype(jnp.int32), low.astype(jnp.int32)])


def project(normed, w_qkv, cosine, sine_table, local_query, local_kv):
    rows = normed.shape[0]
    query_width = local_query * HEAD
    kv_width = local_kv * HEAD
    projected = jnp.dot(normed, w_qkv, preferred_element_type=jnp.float32)
    queries = rotate(
        projected[:, :query_width].reshape(rows, local_query, HEAD), cosine, sine_table
    ).astype(jnp.bfloat16)
    keys = rotate(
        projected[:, query_width : query_width + kv_width].reshape(rows, local_kv, HEAD),
        cosine,
        sine_table,
    ).astype(jnp.bfloat16)
    values = projected[:, query_width + kv_width :].reshape(rows, local_kv, HEAD).astype(jnp.bfloat16)
    return queries, keys, values


def pages_of(keys, values):
    count = keys.shape[0] // PAGE
    local_kv = keys.shape[1]
    key_pages = keys.reshape(count, PAGE, local_kv, HEAD).transpose(0, 2, 1, 3)
    value_pages = values.reshape(count, PAGE, local_kv, HEAD).transpose(0, 2, 1, 3)
    return jnp.stack([key_pages, value_pages], axis=2).reshape(count, local_kv, 2, PAGE * HEAD)


def shards(hidden_in, segment_ids, page_owner, norm_gain, w_qkv, w_out):
    tp_count = lax.axis_size("tp")
    req_count = lax.axis_size("req")
    tp_index = lax.axis_index("tp")
    group_len = segment_ids.shape[0]
    half_len = hidden_in.shape[0]
    local_query = HEADS_Q // tp_count
    local_kv = HEADS_KV // tp_count
    swap = [(0, 1), (1, 0)]
    blocks = half_len // BLOCK
    first = tp_index == 0
    own_start = tp_index * half_len
    other_start = (1 - tp_index) * half_len
    page_count = group_len // PAGE
    positions = positions_of(segment_ids)
    cosine, sine_table = rotary_tables(positions, HEAD)

    def rows_of(array, begin):
        return lax.dynamic_slice_in_dim(array, begin, half_len, axis=0)

    def in_order(own, other):
        return jnp.where(
            first, jnp.concatenate([own, other], axis=0), jnp.concatenate([other, own], axis=0)
        )

    normed_own = normalize(hidden_in, norm_gain)
    normed_other = jnp.concatenate(
        [
            normalize(lax.ppermute(hidden_in[c * BLOCK : (c + 1) * BLOCK], "tp", swap), norm_gain)
            for c in range(blocks)
        ],
        axis=0,
    )
    q_own, k_own, v_own = project(
        normed_own, w_qkv, rows_of(cosine, own_start), rows_of(sine_table, own_start), local_query, local_kv
    )
    q_other, k_other, v_other = project(
        normed_other, w_qkv, rows_of(cosine, other_start), rows_of(sine_table, other_start), local_query, local_kv
    )
    keys = in_order(k_own, k_other)
    values = in_order(v_own, v_other)

    page_data = pages_of(keys, values)
    live_pages = segment_ids[::PAGE] != REQS + 1
    owner_ids = jnp.arange(req_count, dtype=jnp.int32)
    page_numbers = jnp.arange(page_count, dtype=jnp.int32)
    to_owner = (page_owner[None, :] == owner_ids[:, None]) & live_pages[None, :]
    send_index = jnp.where(jnp.any(to_owner, axis=1), jnp.argmax(to_owner, axis=1), page_count)
    payload = page_data.shape[-1]
    tag_block = jnp.broadcast_to(
        (page_numbers + 1).astype(jnp.bfloat16)[:, None, None, None], (page_count, local_kv, 2, 128)
    )
    source_pages = jnp.concatenate(
        [
            jnp.concatenate([page_data, tag_block], axis=3),
            jnp.zeros((1, local_kv, 2, payload + 128), jnp.bfloat16),
        ],
        axis=0,
    )
    send_pages = jnp.take(source_pages, send_index, axis=0, mode="clip")
    received = lax.all_to_all(send_pages, "req", split_axis=0, concat_axis=0, tiled=True)
    received_ids = received[:, 0, 0, payload].astype(jnp.int32) - 1
    from_group = received_ids[None, :] == page_numbers[:, None]
    source_group = jnp.argmax(from_group, axis=1)
    cache_rows = jnp.where(
        jnp.any(from_group, axis=1)[:, None, None, None],
        jnp.take(received, source_group, axis=0, mode="clip")[..., :payload],
        0,
    ).astype(jnp.bfloat16)

    query_heads = in_order(q_own, q_other).transpose(1, 0, 2)
    key_heads = keys.transpose(1, 0, 2)
    value_heads = values.transpose(1, 0, 2)
    link_partner = [
        (r * tp_count + t, (r ^ 2) * tp_count + (tp_count - 1 - t))
        for r in range(req_count)
        for t in range(tp_count)
    ]
    w_out_other = lax.ppermute(w_out, ("req", "tp"), link_partner)

    def attend_half(start):
        meta = block_meta(segment_ids, (start // BLOCK).astype(jnp.int32))
        attended = flash_attention(meta, query_heads, key_heads, value_heads, segment_ids, blocks)
        return attended.transpose(1, 0, 2).reshape(half_len, local_query * HEAD)

    attended_in = lax.ppermute(attend_half(other_start), "tp", swap)
    attended_own = attend_half(own_start)
    projected_out = jnp.dot(attended_own, w_out, preferred_element_type=jnp.float32) + jnp.dot(
        attended_in, w_out_other, preferred_element_type=jnp.float32
    )
    hidden_out = (hidden_in.astype(jnp.float32) + projected_out).astype(jnp.bfloat16)
    return (hidden_out, cache_rows)


def solution(mesh):
    placed = (P(("req", "tp"), None), P("req"), P("req"), P(), P(None, "tp"), P("tp", None))
    return jax.shard_map(
        shards,
        mesh=mesh,
        in_specs=placed,
        out_specs=(P(("req", "tp"), None), P("req", "tp", None, None)),
        check_vma=False,
    )
```

```python
import functools
import math

import jax
import jax.numpy as jnp
from jax import lax
from jax.experimental import pallas as pl
from jax.experimental.pallas import tpu as pltpu
from jax.sharding import PartitionSpec as P

HEAD = 96
HEADS_Q = 8
HEADS_KV = 4
PAGE = 64
REQS = 8
BLOCK = 256
KEY_BLOCK = 512


rotary_base = 100000.0
norm_eps = 1e-05
masked_score = -1e30


def positions_of(segments):
    length = segments.shape[0]
    counter = jnp.arange(length, dtype=jnp.int32)
    previous = jnp.concatenate([segments[:1] - 1, segments[:-1]])
    starts = lax.cummax(jnp.where(segments != previous, counter, 0), axis=0)
    prefix_len = jnp.sum((segments == 0).astype(jnp.int32))
    return counter - starts + jnp.where(segments > 0, prefix_len, 0)


def rotary_tables(positions, width):
    half_width = width // 2
    exponent = jnp.arange(half_width, dtype=jnp.float32) * (2.0 / width)
    inverse = jnp.power(jnp.float32(rotary_base), -exponent)
    angles = positions.astype(jnp.float32)[:, None] * inverse[None, :]
    return (jnp.cos(angles), jnp.sin(angles))


def rotate(vectors, cosine, sine_table):
    half_width = vectors.shape[-1] // 2
    front_half = vectors[..., :half_width]
    second = vectors[..., half_width:]
    cosine = cosine[:, None, :]
    sine_table = sine_table[:, None, :]
    return jnp.concatenate(
        [front_half * cosine - second * sine_table, second * cosine + front_half * sine_table],
        axis=-1,
    )


def normalize(token_rows, gain_vector):
    values = token_rows.astype(jnp.float32)
    inverse_root = lax.rsqrt(jnp.mean(values * values, axis=-1, keepdims=True) + norm_eps)
    return (values * inverse_root * gain_vector.astype(jnp.float32)).astype(jnp.bfloat16)


def flash_kernel(key_width, meta_ref, q_ref, kt_ref, v_ref, segq_ref, segk_ref, o_ref, m_sc, l_sc, acc_sc):
    step = pl.program_id(0)
    query_block = meta_ref[0] + step
    prefix_blocks = meta_ref[1]
    low_block = meta_ref[2 + query_block]
    kv_heads = kt_ref.shape[0]
    group = q_ref.shape[0] // kv_heads
    m_sc[...] = jnp.full(m_sc.shape, masked_score, jnp.float32)
    l_sc[...] = jnp.zeros(l_sc.shape, jnp.float32)
    acc_sc[...] = jnp.zeros(acc_sc.shape, jnp.float32)
    rows = query_block * BLOCK + lax.broadcasted_iota(jnp.int32, (BLOCK, 1), 0)
    query_segments = segq_ref[...]

    def body(key_block, carry):
        @pl.when((key_block < prefix_blocks) | (key_block >= low_block))
        def _():
            start = pl.multiple_of(key_block * key_width, key_width)
            key_segments = segk_ref[:, pl.ds(start, key_width)]
            cols = start + lax.broadcasted_iota(jnp.int32, (1, key_width), 1)
            allowed = (cols <= rows) & ((key_segments == query_segments) | (key_segments == 0))
            bias = jnp.where(allowed, 0.0, masked_score)
            for kv_head in range(kv_heads):
                queries = q_ref[kv_head * group : (kv_head + 1) * group].reshape(group * BLOCK, HEAD)
                scores = jnp.dot(
                    queries, kt_ref[kv_head, :, pl.ds(start, key_width)], preferred_element_type=jnp.float32
                ) * (HEAD ** (-0.5))
                scores = (scores.reshape(group, BLOCK, key_width) + bias[None]).reshape(group * BLOCK, key_width)
                m_prev = m_sc[kv_head]
                m_new = jnp.maximum(m_prev, jnp.max(scores, axis=-1, keepdims=True))
                alpha = jnp.exp(m_prev - m_new)
                weights = jnp.exp(scores - m_new)
                l_sc[kv_head] = alpha * l_sc[kv_head] + jnp.sum(weights, axis=-1, keepdims=True)
                acc_sc[kv_head] = alpha * acc_sc[kv_head] + jnp.dot(
                    weights.astype(jnp.bfloat16),
                    v_ref[kv_head, pl.ds(start, key_width), :],
                    preferred_element_type=jnp.float32,
                )
                m_sc[kv_head] = m_new
        return carry

    lax.fori_loop(0, ((query_block + 1) * BLOCK + key_width - 1) // key_width, body, 0)
    for kv_head in range(kv_heads):
        o_ref[kv_head * group : (kv_head + 1) * group] = (
            (acc_sc[kv_head] / l_sc[kv_head]).reshape(group, BLOCK, HEAD).astype(o_ref.dtype)
        )


def flash_attention(meta, queries, keys, values, segments, steps, key_width=KEY_BLOCK, interpret=False):
    query_heads, length, _ = queries.shape
    kv_heads = keys.shape[0]
    group = query_heads // kv_heads
    grid_spec = pltpu.PrefetchScalarGridSpec(
        num_scalar_prefetch=1,
        grid=(steps,),
        in_specs=[
            pl.BlockSpec((query_heads, BLOCK, HEAD), lambda i, m: (0, m[0] + i, 0)),
            pl.BlockSpec((kv_heads, HEAD, length), lambda i, m: (0, 0, 0)),
            pl.BlockSpec((kv_heads, length, HEAD), lambda i, m: (0, 0, 0)),
            pl.BlockSpec((BLOCK, 1), lambda i, m: (m[0] + i, 0)),
            pl.BlockSpec((1, length), lambda i, m: (0, 0)),
        ],
        out_specs=pl.BlockSpec((query_heads, BLOCK, HEAD), lambda i, m: (0, i, 0)),
        scratch_shapes=[
            pltpu.VMEM((kv_heads, group * BLOCK, 1), jnp.float32),
            pltpu.VMEM((kv_heads, group * BLOCK, 1), jnp.float32),
            pltpu.VMEM((kv_heads, group * BLOCK, HEAD), jnp.float32),
        ],
    )
    return pl.pallas_call(
        functools.partial(flash_kernel, key_width),
        grid_spec=grid_spec,
        out_shape=jax.ShapeDtypeStruct((query_heads, steps * BLOCK, HEAD), jnp.bfloat16),
        compiler_params=pltpu.CompilerParams(dimension_semantics=("arbitrary",)),
        interpret=interpret,
    )(meta, queries, keys.transpose(0, 2, 1), values, segments.reshape(length, 1), segments.reshape(1, length))


def block_meta(segments, base, key_width=KEY_BLOCK):
    length = segments.shape[0]
    counter = jnp.arange(length, dtype=jnp.int32)
    previous = jnp.concatenate([segments[:1] - 1, segments[:-1]])
    starts = lax.cummax(jnp.where(segments != previous, counter, 0), axis=0)
    prefix_len = jnp.sum((segments == 0).astype(jnp.int32))
    prefix_blocks = (prefix_len + key_width - 1) // key_width
    low = starts[::BLOCK] // key_width
    return jnp.concatenate([jnp.stack([base, prefix_blocks]).astype(jnp.int32), low.astype(jnp.int32)])


def project(normed, w_qkv, cosine, sine_table, local_query, local_kv):
    rows = normed.shape[0]
    query_width = local_query * HEAD
    kv_width = local_kv * HEAD
    projected = jnp.dot(normed, w_qkv, preferred_element_type=jnp.float32)
    queries = rotate(
        projected[:, :query_width].reshape(rows, local_query, HEAD), cosine, sine_table
    ).astype(jnp.bfloat16)
    keys = rotate(
        projected[:, query_width : query_width + kv_width].reshape(rows, local_kv, HEAD),
        cosine,
        sine_table,
    ).astype(jnp.bfloat16)
    values = projected[:, query_width + kv_width :].reshape(rows, local_kv, HEAD).astype(jnp.bfloat16)
    return queries, keys, values


def pages_of(keys, values):
    count = keys.shape[0] // PAGE
    local_kv = keys.shape[1]
    key_pages = keys.reshape(count, PAGE, local_kv, HEAD).transpose(0, 2, 1, 3)
    value_pages = values.reshape(count, PAGE, local_kv, HEAD).transpose(0, 2, 1, 3)
    return jnp.stack([key_pages, value_pages], axis=2).reshape(count, local_kv, 2, PAGE * HEAD)


def shards(hidden_in, segment_ids, page_owner, norm_gain, w_qkv, w_out):
    tp_count = lax.axis_size("tp")
    req_count = lax.axis_size("req")
    tp_index = lax.axis_index("tp")
    group_len = segment_ids.shape[0]
    half_len = hidden_in.shape[0]
    local_query = HEADS_Q // tp_count
    local_kv = HEADS_KV // tp_count
    swap = [(0, 1), (1, 0)]
    blocks = half_len // BLOCK
    first = tp_index == 0
    own_start = tp_index * half_len
    other_start = (1 - tp_index) * half_len
    page_count = group_len // PAGE
    positions = positions_of(segment_ids)
    cosine, sine_table = rotary_tables(positions, HEAD)

    def rows_of(array, begin):
        return lax.dynamic_slice_in_dim(array, begin, half_len, axis=0)

    def in_order(own, other):
        return jnp.where(
            first, jnp.concatenate([own, other], axis=0), jnp.concatenate([other, own], axis=0)
        )

    normed_own = normalize(hidden_in, norm_gain)
    normed_other = normalize(
        jnp.concatenate(
            [lax.ppermute(hidden_in[c * BLOCK : (c + 1) * BLOCK], "tp", swap) for c in range(blocks)],
            axis=0,
        ),
        norm_gain,
    )
    q_own, k_own, v_own = project(
        normed_own, w_qkv, rows_of(cosine, own_start), rows_of(sine_table, own_start), local_query, local_kv
    )
    q_other, k_other, v_other = project(
        normed_other, w_qkv, rows_of(cosine, other_start), rows_of(sine_table, other_start), local_query, local_kv
    )
    keys = in_order(k_own, k_other)
    values = in_order(v_own, v_other)

    page_data = pages_of(keys, values)
    live_pages = segment_ids[::PAGE] != REQS + 1
    owner_ids = jnp.arange(req_count, dtype=jnp.int32)
    page_numbers = jnp.arange(page_count, dtype=jnp.int32)
    to_owner = (page_owner[None, :] == owner_ids[:, None]) & live_pages[None, :]
    send_index = jnp.where(jnp.any(to_owner, axis=1), jnp.argmax(to_owner, axis=1), page_count)
    payload = page_data.shape[-1]
    tag_block = jnp.broadcast_to(
        (page_numbers + 1).astype(jnp.bfloat16)[:, None, None, None], (page_count, local_kv, 2, 128)
    )
    source_pages = jnp.concatenate(
        [
            jnp.concatenate([page_data, tag_block], axis=3),
            jnp.zeros((1, local_kv, 2, payload + 128), jnp.bfloat16),
        ],
        axis=0,
    )
    send_pages = jnp.take(source_pages, send_index, axis=0, mode="clip")
    received = lax.all_to_all(send_pages, "req", split_axis=0, concat_axis=0, tiled=True)
    received_ids = received[:, 0, 0, payload].astype(jnp.int32) - 1
    from_group = received_ids[None, :] == page_numbers[:, None]
    source_group = jnp.argmax(from_group, axis=1)
    cache_rows = jnp.where(
        jnp.any(from_group, axis=1)[:, None, None, None],
        jnp.take(received, source_group, axis=0, mode="clip")[..., :payload],
        0,
    ).astype(jnp.bfloat16)

    query_heads = in_order(q_own, q_other).transpose(1, 0, 2)
    key_heads = keys.transpose(1, 0, 2)
    value_heads = values.transpose(1, 0, 2)
    link_partner = [
        (r * tp_count + t, (r ^ 2) * tp_count + (tp_count - 1 - t))
        for r in range(req_count)
        for t in range(tp_count)
    ]
    w_out_other = lax.ppermute(w_out, ("req", "tp"), link_partner)

    def attend_half(start):
        meta = block_meta(segment_ids, (start // BLOCK).astype(jnp.int32))
        attended = flash_attention(meta, query_heads, key_heads, value_heads, segment_ids, blocks)
        return attended.transpose(1, 0, 2).reshape(half_len, local_query * HEAD)

    attended_in = lax.ppermute(attend_half(other_start), "tp", swap)
    attended_own = attend_half(own_start)
    projected_out = jnp.dot(attended_own, w_out, preferred_element_type=jnp.float32) + jnp.dot(
        attended_in, w_out_other, preferred_element_type=jnp.float32
    )
    hidden_out = (hidden_in.astype(jnp.float32) + projected_out).astype(jnp.bfloat16)
    return (hidden_out, cache_rows)


def solution(mesh):
    placed = (P(("req", "tp"), None), P("req"), P("req"), P(), P(None, "tp"), P("tp", None))
    return jax.shard_map(
        shards,
        mesh=mesh,
        in_specs=placed,
        out_specs=(P(("req", "tp"), None), P("req", "tp", None, None)),
        check_vma=False,
    )
```
